256 devices in a mesh: tm: 32 (over y, x, core), tensor: 8 (over z).
Axes of the slice: x: 4, y: 4, z: 8, core: 2. Of those that a mesh axis runs over, the one named last changes fastest.
Arguments:
- features: bfloat16 [32768, 1536], P(('tm', 'tensor')), may hold values from -4 to 4
- frame_mask: int32 [32768], P('tm'), may hold values 0 or 1
- total_length: int32 [1], replicated, may hold values from 24576 to 32768
- norm_gain: float32 [1536], replicated, may hold values from 0.1 to 1.9
- value_weight: bfloat16 [1536, 1536], P(None, 'tensor'), may hold values from -0.15625 to 0.15625
- gate_weight: bfloat16 [1536, 1536], P(None, 'tensor'), may hold values from -0.15625 to 0.15625
- depth_kernel: float32 [31, 1536], P(None, 'tensor'), may hold values from -1 to 1
- batch_gain: float32 [1536], P('tensor'), may hold values from 0.1 to 1.9
- batch_bias: float32 [1536], P('tensor'), may hold values from -2 to 2
- out_weight: bfloat16 [1536, 1536], P('tensor'), may hold values from -0.15625 to 0.15625
- feed_gain: float32 [1536], replicated, may hold values from 0.1 to 1.9
- up_weight: bfloat16 [1536, 6144], P('tm', 'tensor'), may hold values from -0.15625 to 0.15625
- down_weight: bfloat16 [6144, 1536], P('tensor', 'tm'), may hold values from -0.078125 to 0.078125
Outputs:
- encoded: bfloat16 [32768, 1536], P(('tm', 'tensor'))
The draws below stay inside these ranges and needn't reach their ends.
All inputs are finite; a program needn't handle non-finite values. No bound on the sum of `frame_mask` on one device may be relied on, other than what follows from the above.
Results may differ from the reference program's by a relative error of at most 0.0074.
Values may be sent and summed in bfloat16 or wider, within the bound.
No kernel may reach another device: no remote copies, remote signals or barrier semaphores. Data moves between devices by JAX's collectives and lax.ppermute only.
A program may use at most 64 MiB of HBM per device.

```python
import jax
import jax.numpy as jnp
from jax import lax

D = 1536
FF = 6144
KERNEL = 31
FRAMES = 32768


def draw_features(key, part):
    noise_key, line_key = jax.random.split(key)
    ramp = jnp.arange(FRAMES, dtype=jnp.float32) / FRAMES
    noise = 0.15 * jnp.clip(jax.random.normal(noise_key, (FRAMES, D), jnp.float32), -4.0, 4.0)
    strength = 0.8 * (2.0 * ramp - 1.0)
    direction = jnp.clip(jax.random.normal(line_key, (D,), jnp.float32), -3.0, 3.0)
    return jnp.clip(noise + strength[:, None] * direction[None, :], -4.0, 4.0).astype(jnp.bfloat16)


def touch_ends(values, rng, least, high):
    longest = values.shape.index(max(values.shape))
    spots = []
    for shift in (0, 1):
        where = [jax.random.randint(jax.random.fold_in(rng, axis), (), 0, length) for axis, length in enumerate(values.shape)]
        where[longest] = (where[longest] + shift) % values.shape[longest]
        spots.append(tuple(where))
    return values.at[spots[0]].set(least).at[spots[1]].set(high)


def steps_of(stream_key, dims, cuts, low, top_value):
    level, own = 1.0, jax.random.fold_in(stream_key, 6)
    for dim, blocks in cuts:
        steps = jnp.exp(jax.random.uniform(jax.random.fold_in(own, dim), (blocks,), jnp.float32, low / len(cuts), top_value / len(cuts)))
        level = level * jnp.repeat(steps, dims[dim] // blocks).reshape([-1 if axis == dim else 1 for axis in range(len(dims))])
    return level


def gaussian(own_key, shape, scale, most, cuts=(), held_as=jnp.bfloat16):
    values = jax.random.normal(own_key, shape, jnp.float32) * scale
    if len(cuts) > 0:
        values = steps_of(own_key, shape, cuts, -0.22, 0.18) * values
    return jnp.clip(values, min=-most, max=most).astype(held_as)


def setup_inputs(seed: int = 0) -> dict:
    streams_of = jax.random.split(jax.random.key(seed), 14)
    features = draw_features(jax.random.fold_in(streams_of[13], 71), 0)
    frame_mask = touch_ends((jax.random.randint(streams_of[1], (FRAMES,), 0, 16) < 15).astype(jnp.int32), jax.random.fold_in(streams_of[1], 1), 0, 1)
    total_length = jax.random.randint(streams_of[2], (1,), FRAMES - FRAMES // 4, FRAMES + 1).astype(jnp.int32)
    norm_gain = jnp.clip(1.0 + 0.18 * jax.random.normal(streams_of[3], (D,), jnp.float32), 0.1, 1.9)
    value_weight = gaussian(streams_of[4], (D, D), D ** -0.5, 0.15625, ((1, 8),))
    gate_weight = gaussian(streams_of[5], (D, D), D ** -0.5, 0.15625, ((1, 8),))
    depth_kernel = gaussian(streams_of[6], (KERNEL, D), KERNEL ** -0.5, 1.0, ((1, 8),), jnp.float32)
    batch_gain = jnp.clip(1.0 + 0.18 * jax.random.normal(streams_of[7], (D,), jnp.float32), 0.1, 1.9)
    batch_bias = gaussian(streams_of[8], (D,), 0.5, 2.0, ((0, 8),), jnp.float32)
    out_weight = gaussian(streams_of[9], (D, D), D ** -0.5, 0.15625, ((0, 8),))
    feed_gain = jnp.clip(1.0 + 0.18 * jax.random.normal(streams_of[10], (D,), jnp.float32), 0.1, 1.9)
    up_weight = gaussian(streams_of[11], (D, FF), D ** -0.5, 0.15625, ((0, 32), (1, 8)))
    down_weight = gaussian(streams_of[12], (FF, D), FF ** -0.5, 0.078125, ((0, 8), (1, 32)))
    return {"features": features, "frame_mask": frame_mask, "total_length": total_length, "norm_gain": norm_gain, "value_weight": value_weight, "gate_weight": gate_weight, "depth_kernel": depth_kernel, "batch_gain": batch_gain, "batch_bias": batch_bias, "out_weight": out_weight, "feed_gain": feed_gain, "up_weight": up_weight, "down_weight": down_weight}


def layer_norm(rows, gain):
    values = rows.astype(jnp.float32)
    centre = lax.optimization_barrier(jnp.mean(values, axis=-1, keepdims=True))
    spread = lax.optimization_barrier(jnp.mean(jnp.square(values - centre), axis=-1, keepdims=True))
    return (values - centre) * lax.rsqrt(spread + 1e-05) * gain

def reference(features, frame_mask, total_length, norm_gain, value_weight, gate_weight, depth_kernel, batch_gain, batch_bias, out_weight, feed_gain, up_weight, down_weight):
    positions = jnp.arange(FRAMES, dtype=jnp.int32)
    valid = ((frame_mask > 0) & (positions < total_length[0])).astype(jnp.float32)
    normed = layer_norm(features, norm_gain).astype(jnp.bfloat16)
    value = jnp.dot(normed, value_weight, preferred_element_type=jnp.float32)
    gate = jnp.dot(normed, gate_weight, preferred_element_type=jnp.float32)
    glu = (value * jax.nn.sigmoid(gate) * valid[:, None]).astype(jnp.bfloat16)
    reach = KERNEL // 2
    padded = jnp.pad(glu, ((reach, reach), (0, 0)))
    conv = jnp.zeros((FRAMES, D), jnp.float32)
    for tap in range(KERNEL):
        conv = conv + padded[tap:tap + FRAMES].astype(jnp.float32) * depth_kernel[tap]
    count = jnp.sum(valid)
    mean = lax.optimization_barrier(jnp.sum(conv * valid[:, None], axis=0)) / count
    centred = conv - mean
    var = lax.optimization_barrier(jnp.sum(jnp.square(centred) * valid[:, None], axis=0)) / count
    scaled = centred * lax.rsqrt(var + 1e-05) * batch_gain + batch_bias
    swished = (scaled * jax.nn.sigmoid(scaled)).astype(jnp.bfloat16)
    conv_out = jnp.dot(swished, out_weight, preferred_element_type=jnp.float32)
    mid = (features.astype(jnp.float32) + conv_out).astype(jnp.bfloat16)
    feed_normed = layer_norm(mid, feed_gain).astype(jnp.bfloat16)
    pre = jnp.dot(feed_normed, up_weight, preferred_element_type=jnp.float32)
    hidden = (pre * jax.nn.sigmoid(pre)).astype(jnp.bfloat16)
    feed_out = jnp.dot(hidden, down_weight, preferred_element_type=jnp.float32)
    return (mid.astype(jnp.float32) + 0.5 * feed_out).astype(jnp.bfloat16)
```

```python
import jax
import jax.numpy as jnp
from jax import lax
from jax.sharding import PartitionSpec as P

KERNEL = 31


def extended(array, sides, width):
    for axis, dim in sides:
        devices, length = (lax.axis_size(axis), array.shape[dim])
        up = [(i, (i + 1) % devices) for i in range(devices - 1)]
        down = [(j, i) for i, j in up]
        last = lax.slice_in_dim(array, length - width, length, axis=dim)
        initial = lax.slice_in_dim(array, 0, width, axis=dim)
        before = lax.ppermute(last, axis, up)
        after = lax.ppermute(initial, axis, down)
        array = jnp.concatenate([before, array, after], axis=dim)
    return array


def layer_norm(rows, gain):
    values = rows.astype(jnp.float32)
    centre = jnp.mean(values, axis=-1, keepdims=True)
    spread = jnp.mean(jnp.square(values - centre), axis=-1, keepdims=True)
    return (values - centre) * lax.rsqrt(spread + 1e-05) * gain


def merge_moments(low, high):
    n_a, mean_a, m2_a = low[0], low[1], low[2]
    n_b, mean_b, m2_b = high[0], high[1], high[2]
    n = n_a + n_b
    share = jnp.where(n > 0, n_b / jnp.maximum(n, 1.0), 0.0)
    delta = mean_b - mean_a
    mean = mean_a + delta * share
    m2 = m2_a + m2_b + jnp.square(delta) * n_a * share
    return jnp.stack([n, mean, m2])


def moments_over(stats, axis):
    size = lax.axis_size(axis)
    me = lax.axis_index(axis)
    step = 1
    while step < size:
        pairs = [(i, i ^ step) for i in range(size)]
        other = lax.ppermute(stats, axis, pairs)
        mine_low = (me & step) == 0
        low = jnp.where(mine_low, stats, other)
        high = jnp.where(mine_low, other, stats)
        stats = merge_moments(low, high)
        step *= 2
    return stats


def shards(
    features,
    frame_mask,
    total_length,
    norm_gain,
    value_weight,
    gate_weight,
    depth_kernel,
    batch_gain,
    batch_bias,
    out_weight,
    feed_gain,
    up_weight,
    down_weight,
):
    own_rows = features.shape[0]
    block = own_rows * lax.axis_size("tensor")
    positions = lax.axis_index("tm") * block + jnp.arange(block, dtype=jnp.int32)
    valid = ((frame_mask > 0) & (positions < total_length[0])).astype(jnp.float32)
    normed = layer_norm(features, norm_gain).astype(jnp.bfloat16)
    piece = lax.all_gather(normed, "tensor", axis=0, tiled=True)
    up_whole = lax.all_gather(up_weight, "tm", axis=0, tiled=True)
    down_whole = lax.all_gather(down_weight, "tm", axis=1, tiled=True)
    value = jnp.dot(piece, value_weight, preferred_element_type=jnp.float32)
    gate = jnp.dot(piece, gate_weight, preferred_element_type=jnp.float32)
    glu = (value * jax.nn.sigmoid(gate) * valid[:, None]).astype(jnp.bfloat16)
    padded = extended(glu, (("tm", 0),), KERNEL // 2)
    conv = jnp.zeros(glu.shape, jnp.float32)
    for tap in range(KERNEL):
        conv = conv + padded[tap : tap + block].astype(jnp.float32) * depth_kernel[tap]
    count_local = jnp.sum(valid)
    local_sum = jnp.sum(conv * valid[:, None], axis=0)
    local_mean = jnp.where(count_local > 0, local_sum / jnp.maximum(count_local, 1.0), 0.0)
    local_m2 = jnp.sum(jnp.square(conv - local_mean) * valid[:, None], axis=0)
    stats = jnp.stack([jnp.broadcast_to(count_local, local_sum.shape), local_mean, local_m2])
    stats = moments_over(stats, "tm")
    count, mean, m2 = stats[0], stats[1], stats[2]
    centred = conv - mean
    var = m2 / count
    scaled = centred * lax.rsqrt(var + 1e-05) * batch_gain + batch_bias
    swished = (scaled * jax.nn.sigmoid(scaled)).astype(jnp.bfloat16)
    conv_part = jnp.dot(swished, out_weight, preferred_element_type=jnp.float32)
    conv_part, up_whole, down_whole = lax.optimization_barrier((conv_part, up_whole, down_whole))
    conv_out = lax.psum_scatter(
        conv_part.astype(jnp.bfloat16), "tensor", scatter_dimension=0, tiled=True
    ).astype(jnp.float32)
    mid = (features.astype(jnp.float32) + conv_out).astype(jnp.bfloat16)
    feed_normed = layer_norm(mid, feed_gain).astype(jnp.bfloat16)
    feed_block = lax.all_gather(feed_normed, "tensor", axis=0, tiled=True)
    pre = jnp.dot(feed_block, up_whole, preferred_element_type=jnp.float32)
    hidden = (pre * jax.nn.sigmoid(pre)).astype(jnp.bfloat16)
    partial_out = jnp.dot(hidden, down_whole, preferred_element_type=jnp.float32)
    feed_out = lax.psum_scatter(
        partial_out.astype(jnp.bfloat16), "tensor", scatter_dimension=0, tiled=True
    ).astype(jnp.float32)
    return (mid.astype(jnp.float32) + 0.5 * feed_out).astype(jnp.bfloat16)


def solution(mesh):
    placed = (
        P(("tm", "tensor"), None),
        P("tm"),
        P(),
        P(),
        P(None, "tensor"),
        P(None, "tensor"),
        P(None, "tensor"),
        P("tensor"),
        P("tensor"),
        P("tensor", None),
        P(),
        P("tm", "tensor"),
        P("tensor", "tm"),
    )
    return jax.shard_map(
        shards, mesh=mesh, in_specs=placed, out_specs=P(("tm", "tensor"), None), check_vma=False
    )
```

```python
import jax
import jax.numpy as jnp
from jax import lax
from jax.sharding import PartitionSpec as P

KERNEL = 31


def extended(array, sides, width):
    for axis, dim in sides:
        devices, length = (lax.axis_size(axis), array.shape[dim])
        up = [(i, (i + 1) % devices) for i in range(devices - 1)]
        down = [(j, i) for i, j in up]
        last = lax.slice_in_dim(array, length - width, length, axis=dim)
        initial = lax.slice_in_dim(array, 0, width, axis=dim)
        before = lax.ppermute(last, axis, up)
        after = lax.ppermute(initial, axis, down)
        array = jnp.concatenate([before, array, after], axis=dim)
    return array


def layer_norm(rows, gain):
    values = rows.astype(jnp.float32)
    centre = jnp.mean(values, axis=-1, keepdims=True)
    spread = jnp.mean(jnp.square(values - centre), axis=-1, keepdims=True)
    return (values - centre) * lax.rsqrt(spread + 1e-05) * gain


def merge_moments(low, high):
    n_a, mean_a, m2_a = low[0], low[1], low[2]
    n_b, mean_b, m2_b = high[0], high[1], high[2]
    n = n_a + n_b
    share = jnp.where(n > 0, n_b / jnp.maximum(n, 1.0), 0.0)
    delta = mean_b - mean_a
    mean = mean_a + delta * share
    m2 = m2_a + m2_b + jnp.square(delta) * n_a * share
    return jnp.stack([n, mean, m2])


def moments_over(stats, axis):
    size = lax.axis_size(axis)
    me = lax.axis_index(axis)
    step = 1
    while step < size:
        pairs = [(i, i ^ step) for i in range(size)]
        other = lax.ppermute(stats, axis, pairs)
        mine_low = (me & step) == 0
        low = jnp.where(mine_low, stats, other)
        high = jnp.where(mine_low, other, stats)
        stats = merge_moments(low, high)
        step *= 2
    return stats


def gather_torus(pieces, axis):
    size = lax.axis_size(axis)
    cores, xs = 2, 4
    ys = size // (cores * xs)

    def coords(i):
        return i // (cores * xs), (i // cores) % xs, i % cores

    def index(y, x, c):
        return (y * xs + x) * cores + c

    me = lax.axis_index(axis)
    my_c = me % cores
    my_x = (me // cores) % xs
    my_y = me // (cores * xs)

    def shifted(value, move):
        pairs = []
        for i in range(size):
            y, x, c = coords(i)
            pairs.append((i, index(*move(y, x, c))))
        return lax.ppermute(value, axis, pairs)

    def ordered(own, received, mine, count):
        slots = [own] + received
        picks = []
        for j in range(count):
            k = (mine - j) % count
            picked = slots[0]
            for t in range(1, count):
                picked = jnp.where(k == t, slots[t], picked)
            picks.append(picked)
        return picks

    out = []
    for piece in pieces:
        other = shifted(piece, lambda y, x, c: (y, x, 1 - c))
        pair = jnp.concatenate(ordered(piece, [other], my_c, cores), axis=0)
        got = [shifted(pair, lambda y, x, c, d=d: (y, (x + d) % xs, c)) for d in range(1, xs)]
        row = jnp.concatenate(ordered(pair, got, my_x, xs), axis=0)
        got = [shifted(row, lambda y, x, c, d=d: ((y + d) % ys, x, c)) for d in range(1, ys)]
        out.append(jnp.concatenate(ordered(row, got, my_y, ys), axis=0))
    return out


def shards(
    features,
    frame_mask,
    total_length,
    norm_gain,
    value_weight,
    gate_weight,
    depth_kernel,
    batch_gain,
    batch_bias,
    out_weight,
    feed_gain,
    up_weight,
    down_weight,
):
    own_rows = features.shape[0]
    block = own_rows * lax.axis_size("tensor")
    positions = lax.axis_index("tm") * block + jnp.arange(block, dtype=jnp.int32)
    valid = ((frame_mask > 0) & (positions < total_length[0])).astype(jnp.float32)
    normed = layer_norm(features, norm_gain).astype(jnp.bfloat16)
    piece = lax.all_gather(normed, "tensor", axis=0, tiled=True)
    up_whole, down_t = gather_torus([up_weight, down_weight.T], "tm")
    value = jnp.dot(piece, value_weight, preferred_element_type=jnp.float32)
    gate = jnp.dot(piece, gate_weight, preferred_element_type=jnp.float32)
    glu = (value * jax.nn.sigmoid(gate) * valid[:, None]).astype(jnp.bfloat16)
    padded = extended(glu, (("tm", 0),), KERNEL // 2)
    conv = jnp.zeros(glu.shape, jnp.float32)
    for tap in range(KERNEL):
        conv = conv + padded[tap : tap + block].astype(jnp.float32) * depth_kernel[tap]
    count_local = jnp.sum(valid)
    local_sum = jnp.sum(conv * valid[:, None], axis=0)
    local_mean = jnp.where(count_local > 0, local_sum / jnp.maximum(count_local, 1.0), 0.0)
    local_m2 = jnp.sum(jnp.square(conv - local_mean) * valid[:, None], axis=0)
    stats = jnp.stack([jnp.broadcast_to(count_local, local_sum.shape), local_mean, local_m2])
    stats = moments_over(stats, "tm")
    count, mean, m2 = stats[0], stats[1], stats[2]
    centred = conv - mean
    var = m2 / count
    scaled = centred * lax.rsqrt(var + 1e-05) * batch_gain + batch_bias
    swished = (scaled * jax.nn.sigmoid(scaled)).astype(jnp.bfloat16)
    conv_part = jnp.dot(swished, out_weight, preferred_element_type=jnp.float32)
    conv_part, up_whole, down_t = lax.optimization_barrier((conv_part, up_whole, down_t))
    conv_out = lax.psum_scatter(
        conv_part.astype(jnp.bfloat16), "tensor", scatter_dimension=0, tiled=True
    ).astype(jnp.float32)
    mid = (features.astype(jnp.float32) + conv_out).astype(jnp.bfloat16)
    feed_normed = layer_norm(mid, feed_gain).astype(jnp.bfloat16)
    feed_block = lax.all_gather(feed_normed, "tensor", axis=0, tiled=True)
    pre = jnp.dot(feed_block, up_whole, preferred_element_type=jnp.float32)
    hidden = (pre * jax.nn.sigmoid(pre)).astype(jnp.bfloat16)
    partial_out = lax.dot_general(
        hidden, down_t, (((1,), (1,)), ((), ())), preferred_element_type=jnp.float32
    )
    feed_out = lax.psum_scatter(
        partial_out.astype(jnp.bfloat16), "tensor", scatter_dimension=0, tiled=True
    ).astype(jnp.float32)
    return (mid.astype(jnp.float32) + 0.5 * feed_out).astype(jnp.bfloat16)


def solution(mesh):
    placed = (
        P(("tm", "tensor"), None),
        P("tm"),
        P(),
        P(),
        P(None, "tensor"),
        P(None, "tensor"),
        P(None, "tensor"),
        P("tensor"),
        P("tensor"),
        P("tensor", None),
        P(),
        P("tm", "tensor"),
        P("tensor", "tm"),
    )
    return jax.shard_map(
        shards, mesh=mesh, in_specs=placed, out_specs=P(("tm", "tensor"), None), check_vma=False
    )
```

```python
import jax
import jax.numpy as jnp
from jax import lax
from jax.sharding import PartitionSpec as P

KERNEL = 31


def extended(array, sides, width):
    for axis, dim in sides:
        devices, length = (lax.axis_size(axis), array.shape[dim])
        up = [(i, (i + 1) % devices) for i in range(devices - 1)]
        down = [(j, i) for i, j in up]
        last = lax.slice_in_dim(array, length - width, length, axis=dim)
        initial = lax.slice_in_dim(array, 0, width, axis=dim)
        before = lax.ppermute(last, axis, up)
        after = lax.ppermute(initial, axis, down)
        array = jnp.concatenate([before, array, after], axis=dim)
    return array


def layer_norm(rows, gain):
    values = rows.astype(jnp.float32)
    centre = jnp.mean(values, axis=-1, keepdims=True)
    spread = jnp.mean(jnp.square(values - centre), axis=-1, keepdims=True)
    return (values - centre) * lax.rsqrt(spread + 1e-05) * gain


def merge_moments(low, high):
    n_a, mean_a, m2_a = low[0], low[1], low[2]
    n_b, mean_b, m2_b = high[0], high[1], high[2]
    n = n_a + n_b
    share = jnp.where(n > 0, n_b / jnp.maximum(n, 1.0), 0.0)
    delta = mean_b - mean_a
    mean = mean_a + delta * share
    m2 = m2_a + m2_b + jnp.square(delta) * n_a * share
    return jnp.stack([n, mean, m2])


def moments_over(stats, axis):
    size = lax.axis_size(axis)
    me = lax.axis_index(axis)
    step = 1
    while step < size:
        pairs = [(i, i ^ step) for i in range(size)]
        other = lax.ppermute(stats, axis, pairs)
        mine_low = (me & step) == 0
        low = jnp.where(mine_low, stats, other)
        high = jnp.where(mine_low, other, stats)
        stats = merge_moments(low, high)
        step *= 2
    return stats


def gather_torus(pieces, axis):
    size = lax.axis_size(axis)
    cores, xs = 2, 4
    ys = size // (cores * xs)

    def coords(i):
        return i // (cores * xs), (i // cores) % xs, i % cores

    def index(y, x, c):
        return (y * xs + x) * cores + c

    me = lax.axis_index(axis)
    my_c = me % cores
    my_x = (me // cores) % xs
    my_y = me // (cores * xs)

    def shifted(value, move):
        pairs = []
        for i in range(size):
            y, x, c = coords(i)
            pairs.append((i, index(*move(y, x, c))))
        return lax.ppermute(value, axis, pairs)

    def ordered(own, received, mine, count):
        slots = [own] + received
        picks = []
        for j in range(count):
            k = (mine - j) % count
            picked = slots[0]
            for t in range(1, count):
                picked = jnp.where(k == t, slots[t], picked)
            picks.append(picked)
        return picks

    out = []
    for piece in pieces:
        other = shifted(piece, lambda y, x, c: (y, x, 1 - c))
        pair = jnp.concatenate(ordered(piece, [other], my_c, cores), axis=0)
        got = [shifted(pair, lambda y, x, c, d=d: (y, (x + d) % xs, c)) for d in range(1, xs)]
        row = jnp.concatenate(ordered(pair, got, my_x, xs), axis=0)
        got = [shifted(row, lambda y, x, c, d=d: ((y + d) % ys, x, c)) for d in range(1, ys)]
        out.append(jnp.concatenate(ordered(row, got, my_y, ys), axis=0))
    return out


def shards(
    features,
    frame_mask,
    total_length,
    norm_gain,
    value_weight,
    gate_weight,
    depth_kernel,
    batch_gain,
    batch_bias,
    out_weight,
    feed_gain,
    up_weight,
    down_weight,
):
    own_rows = features.shape[0]
    block = own_rows * lax.axis_size("tensor")
    positions = lax.axis_index("tm") * block + jnp.arange(block, dtype=jnp.int32)
    valid = ((frame_mask > 0) & (positions < total_length[0])).astype(jnp.float32)
    normed = layer_norm(features, norm_gain).astype(jnp.bfloat16)
    piece = lax.all_gather(normed, "tensor", axis=0, tiled=True)
    out_whole = lax.all_gather(out_weight, "tensor", axis=0, tiled=True)
    up_whole, down_t = gather_torus([up_weight, down_weight.T], "tm")
    value = jnp.dot(piece, value_weight, preferred_element_type=jnp.float32)
    gate = jnp.dot(piece, gate_weight, preferred_element_type=jnp.float32)
    glu = (value * jax.nn.sigmoid(gate) * valid[:, None]).astype(jnp.bfloat16)
    padded = extended(glu, (("tm", 0),), KERNEL // 2)
    conv = jnp.zeros(glu.shape, jnp.float32)
    for tap in range(KERNEL):
        conv = conv + padded[tap : tap + block].astype(jnp.float32) * depth_kernel[tap]
    count_local = jnp.sum(valid)
    local_sum = jnp.sum(conv * valid[:, None], axis=0)
    local_mean = jnp.where(count_local > 0, local_sum / jnp.maximum(count_local, 1.0), 0.0)
    local_m2 = jnp.sum(jnp.square(conv - local_mean) * valid[:, None], axis=0)
    stats = jnp.stack([jnp.broadcast_to(count_local, local_sum.shape), local_mean, local_m2])
    stats = moments_over(stats, "tm")
    count, mean, m2 = stats[0], stats[1], stats[2]
    centred = conv - mean
    var = m2 / count
    scaled = centred * lax.rsqrt(var + 1e-05) * batch_gain + batch_bias
    swished = (scaled * jax.nn.sigmoid(scaled)).astype(jnp.bfloat16)
    own_swished = lax.all_to_all(swished, "tensor", 0, 1, tiled=True)
    conv_out = jnp.dot(own_swished, out_whole, preferred_element_type=jnp.float32)
    mid = (features.astype(jnp.float32) + conv_out).astype(jnp.bfloat16)
    mid, up_whole, down_t = lax.optimization_barrier((mid, up_whole, down_t))
    feed_normed = layer_norm(mid, feed_gain).astype(jnp.bfloat16)
    feed_block = lax.all_gather(feed_normed, "tensor", axis=0, tiled=True)
    pre = jnp.dot(feed_block, up_whole, preferred_element_type=jnp.float32)
    hidden = (pre * jax.nn.sigmoid(pre)).astype(jnp.bfloat16)
    partial_out = lax.dot_general(
        hidden, down_t, (((1,), (1,)), ((), ())), preferred_element_type=jnp.float32
    )
    feed_out = lax.psum_scatter(
        partial_out.astype(jnp.bfloat16), "tensor", scatter_dimension=0, tiled=True
    ).astype(jnp.float32)
    return (mid.astype(jnp.float32) + 0.5 * feed_out).astype(jnp.bfloat16)


def solution(mesh):
    placed = (
        P(("tm", "tensor"), None),
        P("tm"),
        P(),
        P(),
        P(None, "tensor"),
        P(None, "tensor"),
        P(None, "tensor"),
        P("tensor"),
        P("tensor"),
        P("tensor", None),
        P(),
        P("tm", "tensor"),
        P("tensor", "tm"),
    )
    return jax.shard_map(
        shards, mesh=mesh, in_specs=placed, out_specs=P(("tm", "tensor"), None), check_vma=False
    )
```

```python
import jax
import jax.numpy as jnp
from jax import lax
from jax.sharding import PartitionSpec as P

KERNEL = 31


def extended(array, sides, width):
    for axis, dim in sides:
        devices, length = (lax.axis_size(axis), array.shape[dim])
        up = [(i, (i + 1) % devices) for i in range(devices - 1)]
        down = [(j, i) for i, j in up]
        last = lax.slice_in_dim(array, length - width, length, axis=dim)
        initial = lax.slice_in_dim(array, 0, width, axis=dim)
        before = lax.ppermute(last, axis, up)
        after = lax.ppermute(initial, axis, down)
        array = jnp.concatenate([before, array, after], axis=dim)
    return array


def layer_norm(rows, gain):
    values = rows.astype(jnp.float32)
    centre = jnp.mean(values, axis=-1, keepdims=True)
    spread = jnp.mean(jnp.square(values - centre), axis=-1, keepdims=True)
    return (values - centre) * lax.rsqrt(spread + 1e-05) * gain


def merge_moments(low, high):
    n_a, mean_a, m2_a = low[0], low[1], low[2]
    n_b, mean_b, m2_b = high[0], high[1], high[2]
    n = n_a + n_b
    share = jnp.where(n > 0, n_b / jnp.maximum(n, 1.0), 0.0)
    delta = mean_b - mean_a
    mean = mean_a + delta * share
    m2 = m2_a + m2_b + jnp.square(delta) * n_a * share
    return jnp.stack([n, mean, m2])


def moments_over(stats, axis):
    size = lax.axis_size(axis)
    me = lax.axis_index(axis)
    step = 1
    while step < size:
        pairs = [(i, i ^ step) for i in range(size)]
        other = lax.ppermute(stats, axis, pairs)
        mine_low = (me & step) == 0
        low = jnp.where(mine_low, stats, other)
        high = jnp.where(mine_low, other, stats)
        stats = merge_moments(low, high)
        step *= 2
    return stats


def gather_torus(up_piece, down_piece, axis, tie):
    size = lax.axis_size(axis)
    cores, xs = 2, 4
    ys = size // (cores * xs)

    def coords(i):
        return i // (cores * xs), (i // cores) % xs, i % cores

    def index(y, x, c):
        return (y * xs + x) * cores + c

    me = lax.axis_index(axis)
    my_c = me % cores
    my_x = (me // cores) % xs
    my_y = me // (cores * xs)

    def shifted(value, move):
        pairs = []
        for i in range(size):
            y, x, c = coords(i)
            pairs.append((i, index(*move(y, x, c))))
        return lax.ppermute(value, axis, pairs)

    def ordered(own, received, mine, count):
        slots = [own] + received
        picks = []
        for j in range(count):
            k = (mine - j) % count
            picked = slots[0]
            for t in range(1, count):
                picked = jnp.where(k == t, slots[t], picked)
            picks.append(picked)
        return picks

    partner = lambda y, x, c: (y, x, 1 - c)
    other_up, other_down = shifted((up_piece, down_piece), partner)
    pair_up = jnp.concatenate(ordered(up_piece, [other_up], my_c, cores), axis=0)
    pair_down = jnp.concatenate(ordered(down_piece, [other_down], my_c, cores), axis=0)
    pair = jnp.where(my_c == 0, pair_up, pair_down)
    got = [shifted(pair, lambda y, x, c, d=d: (y, (x + d) % xs, c)) for d in range(1, xs)]
    row = jnp.concatenate(ordered(pair, got, my_x, xs), axis=0)
    got = [shifted(row, lambda y, x, c, d=d: ((y + d) % ys, x, c)) for d in range(1, ys)]
    whole = jnp.concatenate(ordered(row, got, my_y, ys), axis=0)
    whole, tie = lax.optimization_barrier((whole, tie))
    swapped = shifted(whole, partner)
    up_whole = jnp.where(my_c == 0, whole, swapped)
    down_whole = jnp.where(my_c == 0, swapped, whole)
    return up_whole, down_whole, tie


def shards(
    features,
    frame_mask,
    total_length,
    norm_gain,
    value_weight,
    gate_weight,
    depth_kernel,
    batch_gain,
    batch_bias,
    out_weight,
    feed_gain,
    up_weight,
    down_weight,
):
    own_rows = features.shape[0]
    block = own_rows * lax.axis_size("tensor")
    positions = lax.axis_index("tm") * block + jnp.arange(block, dtype=jnp.int32)
    valid = ((frame_mask > 0) & (positions < total_length[0])).astype(jnp.float32)
    normed = layer_norm(features, norm_gain).astype(jnp.bfloat16)
    piece = lax.all_gather(normed, "tensor", axis=0, tiled=True)
    out_whole = lax.all_gather(out_weight, "tensor", axis=0, tiled=True)
    value = jnp.dot(piece, value_weight, preferred_element_type=jnp.float32)
    gate = jnp.dot(piece, gate_weight, preferred_element_type=jnp.float32)
    glu = (value * jax.nn.sigmoid(gate) * valid[:, None]).astype(jnp.bfloat16)
    up_whole, down_t, glu = gather_torus(up_weight, down_weight.T, "tm", glu)
    padded = extended(glu, (("tm", 0),), KERNEL // 2)
    conv = jnp.zeros(glu.shape, jnp.float32)
    for tap in range(KERNEL):
        conv = conv + padded[tap : tap + block].astype(jnp.float32) * depth_kernel[tap]
    count_local = jnp.sum(valid)
    local_sum = jnp.sum(conv * valid[:, None], axis=0)
    local_mean = jnp.where(count_local > 0, local_sum / jnp.maximum(count_local, 1.0), 0.0)
    local_m2 = jnp.sum(jnp.square(conv - local_mean) * valid[:, None], axis=0)
    stats = jnp.stack([jnp.broadcast_to(count_local, local_sum.shape), local_mean, local_m2])
    stats = moments_over(stats, "tm")
    count, mean, m2 = stats[0], stats[1], stats[2]
    centred = conv - mean
    var = m2 / count
    scaled = centred * lax.rsqrt(var + 1e-05) * batch_gain + batch_bias
    swished = (scaled * jax.nn.sigmoid(scaled)).astype(jnp.bfloat16)
    own_swished = lax.all_to_all(swished, "tensor", 0, 1, tiled=True)
    conv_out = jnp.dot(own_swished, out_whole, preferred_element_type=jnp.float32)
    mid = (features.astype(jnp.float32) + conv_out).astype(jnp.bfloat16)
    mid, up_whole, down_t = lax.optimization_barrier((mid, up_whole, down_t))
    feed_normed = layer_norm(mid, feed_gain).astype(jnp.bfloat16)
    feed_block = lax.all_gather(feed_normed, "tensor", axis=0, tiled=True)
    pre = jnp.dot(feed_block, up_whole, preferred_element_type=jnp.float32)
    hidden = (pre * jax.nn.sigmoid(pre)).astype(jnp.bfloat16)
    partial_out = lax.dot_general(
        hidden, down_t, (((1,), (1,)), ((), ())), preferred_element_type=jnp.float32
    )
    feed_out = lax.psum_scatter(
        partial_out.astype(jnp.bfloat16), "tensor", scatter_dimension=0, tiled=True
    ).astype(jnp.float32)
    return (mid.astype(jnp.float32) + 0.5 * feed_out).astype(jnp.bfloat16)


def solution(mesh):
    placed = (
        P(("tm", "tensor"), None),
        P("tm"),
        P(),
        P(),
        P(None, "tensor"),
        P(None, "tensor"),
        P(None, "tensor"),
        P("tensor"),
        P("tensor"),
        P("tensor", None),
        P(),
        P("tm", "tensor"),
        P("tensor", "tm"),
    )
    return jax.shard_map(
        shards, mesh=mesh, in_specs=placed, out_specs=P(("tm", "tensor"), None), check_vma=False
    )
```

```python
import jax
import jax.numpy as jnp
from jax import lax
from jax.sharding import PartitionSpec as P

KERNEL = 31


def extended(array, sides, width):
    for axis, dim in sides:
        devices, length = (lax.axis_size(axis), array.shape[dim])
        up = [(i, (i + 1) % devices) for i in range(devices - 1)]
        down = [(j, i) for i, j in up]
        last = lax.slice_in_dim(array, length - width, length, axis=dim)
        initial = lax.slice_in_dim(array, 0, width, axis=dim)
        before = lax.ppermute(last, axis, up)
        after = lax.ppermute(initial, axis, down)
        array = jnp.concatenate([before, array, after], axis=dim)
    return array


def layer_norm(rows, gain):
    values = rows.astype(jnp.float32)
    centre = jnp.mean(values, axis=-1, keepdims=True)
    spread = jnp.mean(jnp.square(values - centre), axis=-1, keepdims=True)
    return (values - centre) * lax.rsqrt(spread + 1e-05) * gain


def merge_moments(low, high):
    n_a, mean_a, m2_a = low[0], low[1], low[2]
    n_b, mean_b, m2_b = high[0], high[1], high[2]
    n = n_a + n_b
    share = jnp.where(n > 0, n_b / jnp.maximum(n, 1.0), 0.0)
    delta = mean_b - mean_a
    mean = mean_a + delta * share
    m2 = m2_a + m2_b + jnp.square(delta) * n_a * share
    return jnp.stack([n, mean, m2])


def moments_over(stats, axis):
    size = lax.axis_size(axis)
    me = lax.axis_index(axis)
    step = 1
    while step < size:
        pairs = [(i, i ^ step) for i in range(size)]
        other = lax.ppermute(stats, axis, pairs)
        mine_low = (me & step) == 0
        low = jnp.where(mine_low, stats, other)
        high = jnp.where(mine_low, other, stats)
        stats = merge_moments(low, high)
        step *= 2
    return stats


def gather_torus(up_piece, down_piece, axis, tie):
    size = lax.axis_size(axis)
    cores, xs = 2, 4
    ys = size // (cores * xs)

    def coords(i):
        return i // (cores * xs), (i // cores) % xs, i % cores

    def index(y, x, c):
        return (y * xs + x) * cores + c

    me = lax.axis_index(axis)
    my_c = me % cores
    my_x = (me // cores) % xs
    my_y = me // (cores * xs)

    def shifted(value, move):
        pairs = []
        for i in range(size):
            y, x, c = coords(i)
            pairs.append((i, index(*move(y, x, c))))
        return lax.ppermute(value, axis, pairs)

    def ordered(own, received, mine, count):
        slots = [own] + received
        picks = []
        for j in range(count):
            k = (mine - j) % count
            picked = slots[0]
            for t in range(1, count):
                picked = jnp.where(k == t, slots[t], picked)
            picks.append(picked)
        return picks

    partner = lambda y, x, c: (y, x, 1 - c)
    other_up, other_down = shifted((up_piece, down_piece), partner)
    pair_up = jnp.concatenate(ordered(up_piece, [other_up], my_c, cores), axis=0)
    pair_down = jnp.concatenate(ordered(down_piece, [other_down], my_c, cores), axis=0)
    pair = jnp.where(my_c == 0, pair_up, pair_down)
    got = [shifted(pair, lambda y, x, c, d=d: (y, (x + d) % xs, c)) for d in range(1, xs)]
    row = jnp.concatenate(ordered(pair, got, my_x, xs), axis=0)
    got = [shifted(row, lambda y, x, c, d=d: ((y + d) % ys, x, c)) for d in range(1, ys)]
    whole = jnp.concatenate(ordered(row, got, my_y, ys), axis=0)
    whole, tie = lax.optimization_barrier((whole, tie))
    swapped = shifted(whole, partner)
    up_whole = jnp.where(my_c == 0, whole, swapped)
    down_whole = jnp.where(my_c == 0, swapped, whole)
    return up_whole, down_whole, tie


def shards(
    features,
    frame_mask,
    total_length,
    norm_gain,
    value_weight,
    gate_weight,
    depth_kernel,
    batch_gain,
    batch_bias,
    out_weight,
    feed_gain,
    up_weight,
    down_weight,
):
    own_rows = features.shape[0]
    block = own_rows * lax.axis_size("tensor")
    positions = lax.axis_index("tm") * block + jnp.arange(block, dtype=jnp.int32)
    valid = ((frame_mask > 0) & (positions < total_length[0])).astype(jnp.float32)
    feature_block = lax.all_gather(features, "tensor", axis=0, tiled=True)
    piece = layer_norm(feature_block, norm_gain).astype(jnp.bfloat16)
    my_core = lax.axis_index("tm") % 2
    cols = out_weight.shape[1] // 2
    out_half = jnp.where(my_core == 0, out_weight[:, :cols], out_weight[:, cols:])
    out_mine = lax.all_gather(out_half, "tensor", axis=0, tiled=True)
    value = jnp.dot(piece, value_weight, preferred_element_type=jnp.float32)
    gate = jnp.dot(piece, gate_weight, preferred_element_type=jnp.float32)
    glu = (value * jax.nn.sigmoid(gate) * valid[:, None]).astype(jnp.bfloat16)
    up_whole, down_t, glu = gather_torus(up_weight, down_weight.T, "tm", glu)
    padded = extended(glu, (("tm", 0),), KERNEL // 2)
    conv = jnp.zeros(glu.shape, jnp.float32)
    for tap in range(KERNEL):
        conv = conv + padded[tap : tap + block].astype(jnp.float32) * depth_kernel[tap]
    count_local = jnp.sum(valid)
    local_sum = jnp.sum(conv * valid[:, None], axis=0)
    local_mean = jnp.where(count_local > 0, local_sum / jnp.maximum(count_local, 1.0), 0.0)
    local_m2 = jnp.sum(jnp.square(conv - local_mean) * valid[:, None], axis=0)
    stats = jnp.stack([jnp.broadcast_to(count_local, local_sum.shape), local_mean, local_m2])
    stats = moments_over(stats, "tm")
    count, mean, m2 = stats[0], stats[1], stats[2]
    centred = conv - mean
    var = m2 / count
    scaled = centred * lax.rsqrt(var + 1e-05) * batch_gain + batch_bias
    swished = (scaled * jax.nn.sigmoid(scaled)).astype(jnp.bfloat16)
    swished_all = lax.all_gather(swished.T, "tensor", axis=0, tiled=True)
    out_other = lax.ppermute(out_mine, "tm", [(i, i ^ 1) for i in range(lax.axis_size("tm"))])
    left = jnp.where(my_core == 0, out_mine, out_other)
    right = jnp.where(my_core == 0, out_other, out_mine)
    contract = (((0,), (0,)), ((), ()))
    conv_out = jnp.concatenate(
        [
            lax.dot_general(swished_all, left, contract, preferred_element_type=jnp.float32),
            lax.dot_general(swished_all, right, contract, preferred_element_type=jnp.float32),
        ],
        axis=1,
    )
    mid_block = (feature_block.astype(jnp.float32) + conv_out).astype(jnp.bfloat16)
    mid_block, up_whole, down_t = lax.optimization_barrier((mid_block, up_whole, down_t))
    feed_block = layer_norm(mid_block, feed_gain).astype(jnp.bfloat16)
    mid = lax.dynamic_slice_in_dim(mid_block, lax.axis_index("tensor") * own_rows, own_rows, axis=0)
    pre = jnp.dot(feed_block, up_whole, preferred_element_type=jnp.float32)
    hidden = (pre * jax.nn.sigmoid(pre)).astype(jnp.bfloat16)
    partial_out = lax.dot_general(
        hidden, down_t, (((1,), (1,)), ((), ())), preferred_element_type=jnp.float32
    )
    feed_out = lax.psum_scatter(
        partial_out.astype(jnp.bfloat16), "tensor", scatter_dimension=0, tiled=True
    ).astype(jnp.float32)
    return (mid.astype(jnp.float32) + 0.5 * feed_out).astype(jnp.bfloat16)


def solution(mesh):
    placed = (
        P(("tm", "tensor"), None),
        P("tm"),
        P(),
        P(),
        P(None, "tensor"),
        P(None, "tensor"),
        P(None, "tensor"),
        P("tensor"),
        P("tensor"),
        P("tensor", None),
        P(),
        P("tm", "tensor"),
        P("tensor", "tm"),
    )
    return jax.shard_map(
        shards, mesh=mesh, in_specs=placed, out_specs=P(("tm", "tensor"), None), check_vma=False
    )
```

```python
import jax
import jax.numpy as jnp
from jax import lax
from jax.experimental.layout import Layout, with_layout_constraint
from jax.sharding import PartitionSpec as P

KERNEL = 31


def extended(array, sides, width):
    for axis, dim in sides:
        devices, length = (lax.axis_size(axis), array.shape[dim])
        up = [(i, (i + 1) % devices) for i in range(devices - 1)]
        down = [(j, i) for i, j in up]
        last = lax.slice_in_dim(array, length - width, length, axis=dim)
        initial = lax.slice_in_dim(array, 0, width, axis=dim)
        before = lax.ppermute(last, axis, up)
        after = lax.ppermute(initial, axis, down)
        array = jnp.concatenate([before, array, after], axis=dim)
    return array


def layer_norm(rows, gain):
    values = rows.astype(jnp.float32)
    centre = jnp.mean(values, axis=-1, keepdims=True)
    spread = jnp.mean(jnp.square(values - centre), axis=-1, keepdims=True)
    return (values - centre) * lax.rsqrt(spread + 1e-05) * gain


def merge_moments(low, high):
    n_a, mean_a, m2_a = low[0], low[1], low[2]
    n_b, mean_b, m2_b = high[0], high[1], high[2]
    n = n_a + n_b
    share = jnp.where(n > 0, n_b / jnp.maximum(n, 1.0), 0.0)
    delta = mean_b - mean_a
    mean = mean_a + delta * share
    m2 = m2_a + m2_b + jnp.square(delta) * n_a * share
    return jnp.stack([n, mean, m2])


def moments_over(stats, axis):
    size = lax.axis_size(axis)
    me = lax.axis_index(axis)
    step = 1
    while step < size:
        pairs = [(i, i ^ step) for i in range(size)]
        other = lax.ppermute(stats, axis, pairs)
        mine_low = (me & step) == 0
        low = jnp.where(mine_low, stats, other)
        high = jnp.where(mine_low, other, stats)
        stats = merge_moments(low, high)
        step *= 2
    return stats


def gather_torus(up_piece, down_piece, axis, tie):
    size = lax.axis_size(axis)
    cores, xs = 2, 4
    ys = size // (cores * xs)

    def coords(i):
        return i // (cores * xs), (i // cores) % xs, i % cores

    def index(y, x, c):
        return (y * xs + x) * cores + c

    me = lax.axis_index(axis)
    my_c = me % cores
    my_x = (me // cores) % xs
    my_y = me // (cores * xs)

    def shifted(value, move):
        pairs = []
        for i in range(size):
            y, x, c = coords(i)
            pairs.append((i, index(*move(y, x, c))))
        return lax.ppermute(value, axis, pairs)

    def ordered(own, received, mine, count):
        slots = [own] + received
        picks = []
        for j in range(count):
            k = (mine - j) % count
            picked = slots[0]
            for t in range(1, count):
                picked = jnp.where(k == t, slots[t], picked)
            picks.append(picked)
        return picks

    partner = lambda y, x, c: (y, x, 1 - c)
    other_up, other_down = shifted((up_piece, down_piece), partner)
    pair_up = jnp.concatenate(ordered(up_piece, [other_up], my_c, cores), axis=0)
    pair_down = jnp.concatenate(ordered(down_piece, [other_down], my_c, cores), axis=0)
    pair = jnp.where(my_c == 0, pair_up, pair_down)
    got = [shifted(pair, lambda y, x, c, d=d: (y, (x + d) % xs, c)) for d in range(1, xs)]
    row = jnp.concatenate(ordered(pair, got, my_x, xs), axis=0)
    got = [shifted(row, lambda y, x, c, d=d: ((y + d) % ys, x, c)) for d in range(1, ys)]
    whole = jnp.concatenate(ordered(row, got, my_y, ys), axis=0)
    whole, tie = lax.optimization_barrier((whole, tie))
    swapped = shifted(whole, partner)
    up_whole = jnp.where(my_c == 0, whole, swapped)
    down_whole = jnp.where(my_c == 0, swapped, whole)
    return up_whole, down_whole, tie


def shards(
    features,
    frame_mask,
    total_length,
    norm_gain,
    value_weight,
    gate_weight,
    depth_kernel,
    batch_gain,
    batch_bias,
    out_weight,
    feed_gain,
    up_weight,
    down_weight,
):
    own_rows = features.shape[0]
    block = own_rows * lax.axis_size("tensor")
    positions = lax.axis_index("tm") * block + jnp.arange(block, dtype=jnp.int32)
    valid = ((frame_mask > 0) & (positions < total_length[0])).astype(jnp.float32)
    feature_block = lax.all_gather(features, "tensor", axis=0, tiled=True)
    feature_block = with_layout_constraint(feature_block, Layout(major_to_minor=(0, 1)))
    piece = layer_norm(feature_block, norm_gain).astype(jnp.bfloat16)
    my_core = lax.axis_index("tm") % 2
    cols = out_weight.shape[1] // 2
    out_half = jnp.where(my_core == 0, out_weight[:, :cols], out_weight[:, cols:])
    out_mine = lax.all_gather(out_half, "tensor", axis=0, tiled=True)
    value = jnp.dot(piece, value_weight, preferred_element_type=jnp.float32)
    gate = jnp.dot(piece, gate_weight, preferred_element_type=jnp.float32)
    glu = (value * jax.nn.sigmoid(gate) * valid[:, None]).astype(jnp.bfloat16)
    up_whole, down_t, glu = gather_torus(up_weight, down_weight.T, "tm", glu)
    padded = extended(glu, (("tm", 0),), KERNEL // 2)
    conv = jnp.zeros(glu.shape, jnp.float32)
    for tap in range(KERNEL):
        conv = conv + padded[tap : tap + block].astype(jnp.float32) * depth_kernel[tap]
    count_local = jnp.sum(valid)
    local_sum = jnp.sum(conv * valid[:, None], axis=0)
    local_mean = jnp.where(count_local > 0, local_sum / jnp.maximum(count_local, 1.0), 0.0)
    local_m2 = jnp.sum(jnp.square(conv - local_mean) * valid[:, None], axis=0)
    stats = jnp.stack([jnp.broadcast_to(count_local, local_sum.shape), local_mean, local_m2])
    stats = moments_over(stats, "tm")
    count, mean, m2 = stats[0], stats[1], stats[2]
    centred = conv - mean
    var = m2 / count
    scaled = centred * lax.rsqrt(var + 1e-05) * batch_gain + batch_bias
    swished = (scaled * jax.nn.sigmoid(scaled)).astype(jnp.bfloat16)
    swished_all = lax.all_gather(swished, "tensor", axis=1, tiled=True)
    out_other = lax.ppermute(out_mine, "tm", [(i, i ^ 1) for i in range(lax.axis_size("tm"))])
    left = jnp.where(my_core == 0, out_mine, out_other)
    right = jnp.where(my_core == 0, out_other, out_mine)
    contract = (((1,), (0,)), ((), ()))
    conv_out = jnp.concatenate(
        [
            lax.dot_general(swished_all, left, contract, preferred_element_type=jnp.float32),
            lax.dot_general(swished_all, right, contract, preferred_element_type=jnp.float32),
        ],
        axis=1,
    )
    mid_block = (feature_block.astype(jnp.float32) + conv_out).astype(jnp.bfloat16)
    mid_block, up_whole, down_t = lax.optimization_barrier((mid_block, up_whole, down_t))
    feed_block = layer_norm(mid_block, feed_gain).astype(jnp.bfloat16)
    mid = lax.dynamic_slice_in_dim(mid_block, lax.axis_index("tensor") * own_rows, own_rows, axis=0)
    pre = jnp.dot(feed_block, up_whole, preferred_element_type=jnp.float32)
    hidden = (pre * jax.nn.sigmoid(pre)).astype(jnp.bfloat16)
    partial_out = lax.dot_general(
        hidden, down_t, (((1,), (1,)), ((), ())), preferred_element_type=jnp.float32
    )
    feed_out = lax.psum_scatter(
        partial_out.astype(jnp.bfloat16), "tensor", scatter_dimension=0, tiled=True
    ).astype(jnp.float32)
    return (mid.astype(jnp.float32) + 0.5 * feed_out).astype(jnp.bfloat16)


def solution(mesh):
    placed = (
        P(("tm", "tensor"), None),
        P("tm"),
        P(),
        P(),
        P(None, "tensor"),
        P(None, "tensor"),
        P(None, "tensor"),
        P("tensor"),
        P("tensor"),
        P("tensor", None),
        P(),
        P("tm", "tensor"),
        P("tensor", "tm"),
    )
    return jax.shard_map(
        shards, mesh=mesh, in_specs=placed, out_specs=P(("tm", "tensor"), None), check_vma=False
    )
```

```python
import jax
import jax.numpy as jnp
from jax import lax
from jax.experimental.layout import Layout, with_layout_constraint
from jax.sharding import PartitionSpec as P

KERNEL = 31


def extended(array, sides, width):
    for axis, dim in sides:
        devices, length = (lax.axis_size(axis), array.shape[dim])
        up = [(i, (i + 1) % devices) for i in range(devices - 1)]
        down = [(j, i) for i, j in up]
        last = lax.slice_in_dim(array, length - width, length, axis=dim)
        initial = lax.slice_in_dim(array, 0, width, axis=dim)
        before = lax.ppermute(last, axis, up)
        after = lax.ppermute(initial, axis, down)
        array = jnp.concatenate([before, array, after], axis=dim)
    return array


def layer_norm(rows, gain):
    values = rows.astype(jnp.float32)
    centre = jnp.mean(values, axis=-1, keepdims=True)
    spread = jnp.mean(jnp.square(values - centre), axis=-1, keepdims=True)
    return (values - centre) * lax.rsqrt(spread + 1e-05) * gain


def merge_moments(low, high):
    n_a, mean_a, m2_a = low[0], low[1], low[2]
    n_b, mean_b, m2_b = high[0], high[1], high[2]
    n = n_a + n_b
    share = jnp.where(n > 0, n_b / jnp.maximum(n, 1.0), 0.0)
    delta = mean_b - mean_a
    mean = mean_a + delta * share
    m2 = m2_a + m2_b + jnp.square(delta) * n_a * share
    return jnp.stack([n, mean, m2])


def moments_over(stats, axis):
    size = lax.axis_size(axis)
    me = lax.axis_index(axis)
    step = 1
    while step < size:
        pairs = [(i, i ^ step) for i in range(size)]
        other = lax.ppermute(stats, axis, pairs)
        mine_low = (me & step) == 0
        low = jnp.where(mine_low, stats, other)
        high = jnp.where(mine_low, other, stats)
        stats = merge_moments(low, high)
        step *= 2
    return stats


def gather_torus(up_piece, down_piece, axis, tie):
    size = lax.axis_size(axis)
    cores, xs = 2, 4
    ys = size // (cores * xs)

    def coords(i):
        return i // (cores * xs), (i // cores) % xs, i % cores

    def index(y, x, c):
        return (y * xs + x) * cores + c

    me = lax.axis_index(axis)
    my_c = me % cores
    my_x = (me // cores) % xs
    my_y = me // (cores * xs)

    def shifted(value, move):
        pairs = []
        for i in range(size):
            y, x, c = coords(i)
            pairs.append((i, index(*move(y, x, c))))
        return lax.ppermute(value, axis, pairs)

    def ordered(own, received, mine, count):
        slots = [own] + received
        picks = []
        for j in range(count):
            k = (mine - j) % count
            picked = slots[0]
            for t in range(1, count):
                picked = jnp.where(k == t, slots[t], picked)
            picks.append(picked)
        return picks

    partner = lambda y, x, c: (y, x, 1 - c)
    other_up, other_down = shifted((up_piece, down_piece), partner)
    pair_up = jnp.concatenate(ordered(up_piece, [other_up], my_c, cores), axis=0)
    pair_down = jnp.concatenate(ordered(down_piece, [other_down], my_c, cores), axis=0)
    pair = jnp.where(my_c == 0, pair_up, pair_down)
    got = [shifted(pair, lambda y, x, c, d=d: (y, (x + d) % xs, c)) for d in range(1, xs)]
    row = jnp.concatenate(ordered(pair, got, my_x, xs), axis=0)
    got = [shifted(row, lambda y, x, c, d=d: ((y + d) % ys, x, c)) for d in range(1, ys)]
    whole = jnp.concatenate(ordered(row, got, my_y, ys), axis=0)
    whole, tie = lax.optimization_barrier((whole, tie))
    swapped = shifted(whole, partner)
    up_whole = jnp.where(my_c == 0, whole, swapped)
    down_whole = jnp.where(my_c == 0, swapped, whole)
    return up_whole, down_whole, tie


def moments_torus(stats, axis):
    size = lax.axis_size(axis)
    cores, xs = 2, 4
    ys = size // (cores * xs)
    me = lax.axis_index(axis)
    my_c = me % cores
    my_x = (me // cores) % xs
    my_y = me // (cores * xs)

    def index(y, x, c):
        return (y * xs + x) * cores + c

    def shifted(value, move):
        pairs = []
        for i in range(size):
            y, x, c = i // (cores * xs), (i // cores) % xs, i % cores
            pairs.append((i, index(*move(y, x, c))))
        return lax.ppermute(value, axis, pairs)

    def merged_ring(value, mine, count, move):
        got = [value] + [shifted(value, lambda y, x, c, d=d: move(y, x, c, d)) for d in range(1, count)]
        slots = []
        for j in range(count):
            k = (mine - j) % count
            picked = got[0]
            for t in range(1, count):
                picked = jnp.where(k == t, got[t], picked)
            slots.append(picked)
        total = slots[0]
        for j in range(1, count):
            total = merge_moments(total, slots[j])
        return total

    stats = merged_ring(stats, my_c, cores, lambda y, x, c, d: (y, x, (c + d) % cores))
    stats = merged_ring(stats, my_x, xs, lambda y, x, c, d: (y, (x + d) % xs, c))
    stats = merged_ring(stats, my_y, ys, lambda y, x, c, d: ((y + d) % ys, x, c))
    return stats


def shards(
    features,
    frame_mask,
    total_length,
    norm_gain,
    value_weight,
    gate_weight,
    depth_kernel,
    batch_gain,
    batch_bias,
    out_weight,
    feed_gain,
    up_weight,
    down_weight,
):
    own_rows = features.shape[0]
    block = own_rows * lax.axis_size("tensor")
    positions = lax.axis_index("tm") * block + jnp.arange(block, dtype=jnp.int32)
    valid = ((frame_mask > 0) & (positions < total_length[0])).astype(jnp.float32)
    feature_block = lax.all_gather(features, "tensor", axis=0, tiled=True)
    feature_block = with_layout_constraint(feature_block, Layout(major_to_minor=(0, 1)))
    piece = layer_norm(feature_block, norm_gain).astype(jnp.bfloat16)
    my_core = lax.axis_index("tm") % 2
    cols = out_weight.shape[1] // 2
    out_half = jnp.where(my_core == 0, out_weight[:, :cols], out_weight[:, cols:])
    out_mine = lax.all_gather(out_half, "tensor", axis=0, tiled=True)
    value = jnp.dot(piece, value_weight, preferred_element_type=jnp.float32)
    gate = jnp.dot(piece, gate_weight, preferred_element_type=jnp.float32)
    glu = (value * jax.nn.sigmoid(gate) * valid[:, None]).astype(jnp.bfloat16)
    up_whole, down_t, glu = gather_torus(up_weight, down_weight.T, "tm", glu)
    padded = extended(glu, (("tm", 0),), KERNEL // 2)
    conv = jnp.zeros(glu.shape, jnp.float32)
    for tap in range(KERNEL):
        conv = conv + padded[tap : tap + block].astype(jnp.float32) * depth_kernel[tap]
    count_local = jnp.sum(valid)
    local_sum = jnp.sum(conv * valid[:, None], axis=0)
    local_mean = jnp.where(count_local > 0, local_sum / jnp.maximum(count_local, 1.0), 0.0)
    local_m2 = jnp.sum(jnp.square(conv - local_mean) * valid[:, None], axis=0)
    stats = jnp.stack([jnp.broadcast_to(count_local, local_sum.shape), local_mean, local_m2])
    stats = moments_torus(stats, "tm")
    count, mean, m2 = stats[0], stats[1], stats[2]
    centred = conv - mean
    var = m2 / count
    scaled = centred * lax.rsqrt(var + 1e-05) * batch_gain + batch_bias
    swished = (scaled * jax.nn.sigmoid(scaled)).astype(jnp.bfloat16)
    swished_all = lax.all_gather(swished, "tensor", axis=1, tiled=True)
    out_other = lax.ppermute(out_mine, "tm", [(i, i ^ 1) for i in range(lax.axis_size("tm"))])
    left = jnp.where(my_core == 0, out_mine, out_other)
    right = jnp.where(my_core == 0, out_other, out_mine)
    contract = (((1,), (0,)), ((), ()))
    conv_out = jnp.concatenate(
        [
            lax.dot_general(swished_all, left, contract, preferred_element_type=jnp.float32),
            lax.dot_general(swished_all, right, contract, preferred_element_type=jnp.float32),
        ],
        axis=1,
    )
    mid_block = (feature_block.astype(jnp.float32) + conv_out).astype(jnp.bfloat16)
    mid_block, up_whole, down_t = lax.optimization_barrier((mid_block, up_whole, down_t))
    feed_block = layer_norm(mid_block, feed_gain).astype(jnp.bfloat16)
    mid = lax.dynamic_slice_in_dim(mid_block, lax.axis_index("tensor") * own_rows, own_rows, axis=0)
    pre = jnp.dot(feed_block, up_whole, preferred_element_type=jnp.float32)
    hidden = (pre * jax.nn.sigmoid(pre)).astype(jnp.bfloat16)
    partial_out = lax.dot_general(
        hidden, down_t, (((1,), (1,)), ((), ())), preferred_element_type=jnp.float32
    )
    feed_out = lax.psum_scatter(
        partial_out.astype(jnp.bfloat16), "tensor", scatter_dimension=0, tiled=True
    ).astype(jnp.float32)
    return (mid.astype(jnp.float32) + 0.5 * feed_out).astype(jnp.bfloat16)


def solution(mesh):
    placed = (
        P(("tm", "tensor"), None),
        P("tm"),
        P(),
        P(),
        P(None, "tensor"),
        P(None, "tensor"),
        P(None, "tensor"),
        P("tensor"),
        P("tensor"),
        P("tensor", None),
        P(),
        P("tm", "tensor"),
        P("tensor", "tm"),
    )
    return jax.shard_map(
        shards, mesh=mesh, in_specs=placed, out_specs=P(("tm", "tensor"), None), check_vma=False
    )
```

```python
import jax
import jax.numpy as jnp
from jax import lax
from jax.experimental.layout import Layout, with_layout_constraint
from jax.sharding import PartitionSpec as P

KERNEL = 31


def extended(array, sides, width):
    for axis, dim in sides:
        devices, length = (lax.axis_size(axis), array.shape[dim])
        up = [(i, (i + 1) % devices) for i in range(devices - 1)]
        down = [(j, i) for i, j in up]
        last = lax.slice_in_dim(array, length - width, length, axis=dim)
        initial = lax.slice_in_dim(array, 0, width, axis=dim)
        before = lax.ppermute(last, axis, up)
        after = lax.ppermute(initial, axis, down)
        array = jnp.concatenate([before, array, after], axis=dim)
    return array


def layer_norm(rows, gain):
    values = rows.astype(jnp.float32)
    centre = jnp.mean(values, axis=-1, keepdims=True)
    spread = jnp.mean(jnp.square(values - centre), axis=-1, keepdims=True)
    return (values - centre) * lax.rsqrt(spread + 1e-05) * gain


def merge_moments(low, high):
    n_a, mean_a, m2_a = low[0], low[1], low[2]
    n_b, mean_b, m2_b = high[0], high[1], high[2]
    n = n_a + n_b
    share = jnp.where(n > 0, n_b / jnp.maximum(n, 1.0), 0.0)
    delta = mean_b - mean_a
    mean = mean_a + delta * share
    m2 = m2_a + m2_b + jnp.square(delta) * n_a * share
    return jnp.stack([n, mean, m2])


def moments_over(stats, axis):
    size = lax.axis_size(axis)
    me = lax.axis_index(axis)
    step = 1
    while step < size:
        pairs = [(i, i ^ step) for i in range(size)]
        other = lax.ppermute(stats, axis, pairs)
        mine_low = (me & step) == 0
        low = jnp.where(mine_low, stats, other)
        high = jnp.where(mine_low, other, stats)
        stats = merge_moments(low, high)
        step *= 2
    return stats


def gather_torus(up_piece, down_piece, axis, tie):
    size = lax.axis_size(axis)
    cores, xs = 2, 4
    ys = size // (cores * xs)

    def coords(i):
        return i // (cores * xs), (i // cores) % xs, i % cores

    def index(y, x, c):
        return (y * xs + x) * cores + c

    me = lax.axis_index(axis)
    my_c = me % cores
    my_x = (me // cores) % xs
    my_y = me // (cores * xs)

    def shifted(value, move):
        pairs = []
        for i in range(size):
            y, x, c = coords(i)
            pairs.append((i, index(*move(y, x, c))))
        return lax.ppermute(value, axis, pairs)

    def ordered(own, received, mine, count):
        slots = [own] + received
        picks = []
        for j in range(count):
            k = (mine - j) % count
            picked = slots[0]
            for t in range(1, count):
                picked = jnp.where(k == t, slots[t], picked)
            picks.append(picked)
        return picks

    partner = lambda y, x, c: (y, x, 1 - c)
    other_up, other_down = shifted((up_piece, down_piece), partner)
    pair_up = jnp.concatenate(ordered(up_piece, [other_up], my_c, cores), axis=0)
    pair_down = jnp.concatenate(ordered(down_piece, [other_down], my_c, cores), axis=0)
    pair = jnp.where(my_c == 0, pair_up, pair_down)
    got = [shifted(pair, lambda y, x, c, d=d: (y, (x + d) % xs, c)) for d in range(1, xs)]
    row = jnp.concatenate(ordered(pair, got, my_x, xs), axis=0)
    got = [shifted(row, lambda y, x, c, d=d: ((y + d) % ys, x, c)) for d in range(1, ys)]
    whole = jnp.concatenate(ordered(row, got, my_y, ys), axis=0)
    whole, tie = lax.optimization_barrier((whole, tie))
    swapped = shifted(whole, partner)
    up_whole = jnp.where(my_c == 0, whole, swapped)
    down_whole = jnp.where(my_c == 0, swapped, whole)
    return up_whole, down_whole, tie


def gather_by_all_to_all(up_piece, down_piece, axis):
    size = lax.axis_size(axis)
    sent = jnp.stack([up_piece, down_piece] * (size // 2))
    got = lax.all_to_all(sent, axis, 0, 0, tiled=True)
    return got.reshape(size * up_piece.shape[0], up_piece.shape[1])


def shards(
    features,
    frame_mask,
    total_length,
    norm_gain,
    value_weight,
    gate_weight,
    depth_kernel,
    batch_gain,
    batch_bias,
    out_weight,
    feed_gain,
    up_weight,
    down_weight,
):
    own_rows = features.shape[0]
    block = own_rows * lax.axis_size("tensor")
    positions = lax.axis_index("tm") * block + jnp.arange(block, dtype=jnp.int32)
    valid = ((frame_mask > 0) & (positions < total_length[0])).astype(jnp.float32)
    feature_block = lax.all_gather(features, "tensor", axis=0, tiled=True)
    feature_block = with_layout_constraint(feature_block, Layout(major_to_minor=(0, 1)))
    piece = layer_norm(feature_block, norm_gain).astype(jnp.bfloat16)
    my_core = lax.axis_index("tm") % 2
    cols = out_weight.shape[1] // 2
    out_half = jnp.where(my_core == 0, out_weight[:, :cols], out_weight[:, cols:])
    out_mine = lax.all_gather(out_half, "tensor", axis=0, tiled=True)
    value = jnp.dot(piece, value_weight, preferred_element_type=jnp.float32)
    gate = jnp.dot(piece, gate_weight, preferred_element_type=jnp.float32)
    glu = (value * jax.nn.sigmoid(gate) * valid[:, None]).astype(jnp.bfloat16)
    padded = extended(glu, (("tm", 0),), KERNEL // 2)
    conv = jnp.zeros(glu.shape, jnp.float32)
    for tap in range(KERNEL):
        conv = conv + padded[tap : tap + block].astype(jnp.float32) * depth_kernel[tap]
    count_local = jnp.sum(valid)
    local_sum = jnp.sum(conv * valid[:, None], axis=0)
    local_mean = jnp.where(count_local > 0, local_sum / jnp.maximum(count_local, 1.0), 0.0)
    local_m2 = jnp.sum(jnp.square(conv - local_mean) * valid[:, None], axis=0)
    stats = jnp.stack([jnp.broadcast_to(count_local, local_sum.shape), local_mean, local_m2])
    stats = moments_over(stats, "tm")
    count, mean, m2 = stats[0], stats[1], stats[2]
    centred = conv - mean
    var = m2 / count
    scaled = centred * lax.rsqrt(var + 1e-05) * batch_gain + batch_bias
    swished = (scaled * jax.nn.sigmoid(scaled)).astype(jnp.bfloat16)
    swished_all = lax.all_gather(swished, "tensor", axis=1, tiled=True)
    ff_mine = gather_by_all_to_all(up_weight, down_weight.T, "tm")
    swap = [(i, i ^ 1) for i in range(lax.axis_size("tm"))]
    out_other, ff_other = lax.ppermute(jnp.stack([out_mine, ff_mine]), "tm", swap)
    up_whole = jnp.where(my_core == 0, ff_mine, ff_other)
    down_t = jnp.where(my_core == 0, ff_other, ff_mine)
    left = jnp.where(my_core == 0, out_mine, out_other)
    right = jnp.where(my_core == 0, out_other, out_mine)
    contract = (((1,), (0,)), ((), ()))
    conv_out = jnp.concatenate(
        [
            lax.dot_general(swished_all, left, contract, preferred_element_type=jnp.float32),
            lax.dot_general(swished_all, right, contract, preferred_element_type=jnp.float32),
        ],
        axis=1,
    )
    mid_block = (feature_block.astype(jnp.float32) + conv_out).astype(jnp.bfloat16)
    mid_block, up_whole, down_t = lax.optimization_barrier((mid_block, up_whole, down_t))
    feed_block = layer_norm(mid_block, feed_gain).astype(jnp.bfloat16)
    mid = lax.dynamic_slice_in_dim(mid_block, lax.axis_index("tensor") * own_rows, own_rows, axis=0)
    pre = jnp.dot(feed_block, up_whole, preferred_element_type=jnp.float32)
    hidden = (pre * jax.nn.sigmoid(pre)).astype(jnp.bfloat16)
    partial_out = lax.dot_general(
        hidden, down_t, (((1,), (1,)), ((), ())), preferred_element_type=jnp.float32
    )
    feed_out = lax.psum_scatter(
        partial_out.astype(jnp.bfloat16), "tensor", scatter_dimension=0, tiled=True
    ).astype(jnp.float32)
    return (mid.astype(jnp.float32) + 0.5 * feed_out).astype(jnp.bfloat16)


def solution(mesh):
    placed = (
        P(("tm", "tensor"), None),
        P("tm"),
        P(),
        P(),
        P(None, "tensor"),
        P(None, "tensor"),
        P(None, "tensor"),
        P("tensor"),
        P("tensor"),
        P("tensor", None),
        P(),
        P("tm", "tensor"),
        P("tensor", "tm"),
    )
    return jax.shard_map(
        shards, mesh=mesh, in_specs=placed, out_specs=P(("tm", "tensor"), None), check_vma=False
    )
```

```python
import jax
import jax.numpy as jnp
from jax import lax
from jax.experimental.layout import Layout, with_layout_constraint
from jax.sharding import PartitionSpec as P

KERNEL = 31


def extended(array, sides, width):
    for axis, dim in sides:
        devices, length = (lax.axis_size(axis), array.shape[dim])
        up = [(i, (i + 1) % devices) for i in range(devices - 1)]
        down = [(j, i) for i, j in up]
        last = lax.slice_in_dim(array, length - width, length, axis=dim)
        initial = lax.slice_in_dim(array, 0, width, axis=dim)
        before = lax.ppermute(last, axis, up)
        after = lax.ppermute(initial, axis, down)
        array = jnp.concatenate([before, array, after], axis=dim)
    return array


def layer_norm(rows, gain):
    values = rows.astype(jnp.float32)
    centre = jnp.mean(values, axis=-1, keepdims=True)
    spread = jnp.mean(jnp.square(values - centre), axis=-1, keepdims=True)
    return (values - centre) * lax.rsqrt(spread + 1e-05) * gain


def merge_moments(low, high):
    n_a, mean_a, m2_a = low[0], low[1], low[2]
    n_b, mean_b, m2_b = high[0], high[1], high[2]
    n = n_a + n_b
    share = jnp.where(n > 0, n_b / jnp.maximum(n, 1.0), 0.0)
    delta = mean_b - mean_a
    mean = mean_a + delta * share
    m2 = m2_a + m2_b + jnp.square(delta) * n_a * share
    return jnp.stack([n, mean, m2])


def moments_over(stats, axis):
    size = lax.axis_size(axis)
    me = lax.axis_index(axis)
    step = 1
    while step < size:
        pairs = [(i, i ^ step) for i in range(size)]
        other = lax.ppermute(stats, axis, pairs)
        mine_low = (me & step) == 0
        low = jnp.where(mine_low, stats, other)
        high = jnp.where(mine_low, other, stats)
        stats = merge_moments(low, high)
        step *= 2
    return stats


def gather_torus(up_piece, down_piece, axis, tie):
    size = lax.axis_size(axis)
    cores, xs = 2, 4
    ys = size // (cores * xs)

    def coords(i):
        return i // (cores * xs), (i // cores) % xs, i % cores

    def index(y, x, c):
        return (y * xs + x) * cores + c

    me = lax.axis_index(axis)
    my_c = me % cores
    my_x = (me // cores) % xs
    my_y = me // (cores * xs)

    def shifted(value, move):
        pairs = []
        for i in range(size):
            y, x, c = coords(i)
            pairs.append((i, index(*move(y, x, c))))
        return lax.ppermute(value, axis, pairs)

    def ordered(own, received, mine, count):
        slots = [own] + received
        picks = []
        for j in range(count):
            k = (mine - j) % count
            picked = slots[0]
            for t in range(1, count):
                picked = jnp.where(k == t, slots[t], picked)
            picks.append(picked)
        return picks

    partner = lambda y, x, c: (y, x, 1 - c)
    other_up, other_down = shifted((up_piece, down_piece), partner)
    pair_up = jnp.concatenate(ordered(up_piece, [other_up], my_c, cores), axis=0)
    pair_down = jnp.concatenate(ordered(down_piece, [other_down], my_c, cores), axis=0)
    pair = jnp.where(my_c == 0, pair_up, pair_down)
    got = [shifted(pair, lambda y, x, c, d=d: (y, (x + d) % xs, c)) for d in range(1, xs)]
    row = jnp.concatenate(ordered(pair, got, my_x, xs), axis=0)
    got = [shifted(row, lambda y, x, c, d=d: ((y + d) % ys, x, c)) for d in range(1, ys)]
    whole = jnp.concatenate(ordered(row, got, my_y, ys), axis=0)
    whole, tie = lax.optimization_barrier((whole, tie))
    swapped = shifted(whole, partner)
    up_whole = jnp.where(my_c == 0, whole, swapped)
    down_whole = jnp.where(my_c == 0, swapped, whole)
    return up_whole, down_whole, tie


def gather_by_all_to_all(up_piece, down_piece, axis):
    size = lax.axis_size(axis)
    sent = jnp.stack([up_piece, down_piece] * (size // 2))
    got = lax.all_to_all(sent, axis, 0, 0, tiled=True)
    return got.reshape(size * up_piece.shape[0], up_piece.shape[1])


def shards(
    features,
    frame_mask,
    total_length,
    norm_gain,
    value_weight,
    gate_weight,
    depth_kernel,
    batch_gain,
    batch_bias,
    out_weight,
    feed_gain,
    up_weight,
    down_weight,
):
    own_rows = features.shape[0]
    block = own_rows * lax.axis_size("tensor")
    positions = lax.axis_index("tm") * block + jnp.arange(block, dtype=jnp.int32)
    valid = ((frame_mask > 0) & (positions < total_length[0])).astype(jnp.float32)
    feature_block = lax.all_gather(features, "tensor", axis=0, tiled=True)
    feature_block = with_layout_constraint(feature_block, Layout(major_to_minor=(0, 1)))
    piece = layer_norm(feature_block, norm_gain).astype(jnp.bfloat16)
    my_core = lax.axis_index("tm") % 2
    cols = out_weight.shape[1] // 2
    out_half = jnp.where(my_core == 0, out_weight[:, :cols], out_weight[:, cols:])
    out_mine = lax.all_gather(out_half, "tensor", axis=0, tiled=True)
    value = jnp.dot(piece, value_weight, preferred_element_type=jnp.float32)
    gate = jnp.dot(piece, gate_weight, preferred_element_type=jnp.float32)
    glu = (value * jax.nn.sigmoid(gate) * valid[:, None]).astype(jnp.bfloat16)
    ff_mine = gather_by_all_to_all(up_weight, down_weight.T, "tm")
    ff_mine, glu = lax.optimization_barrier((ff_mine, glu))
    padded = extended(glu, (("tm", 0),), KERNEL // 2)
    conv = jnp.zeros(glu.shape, jnp.float32)
    for tap in range(KERNEL):
        conv = conv + padded[tap : tap + block].astype(jnp.float32) * depth_kernel[tap]
    count_local = jnp.sum(valid)
    local_sum = jnp.sum(conv * valid[:, None], axis=0)
    local_mean = jnp.where(count_local > 0, local_sum / jnp.maximum(count_local, 1.0), 0.0)
    local_m2 = jnp.sum(jnp.square(conv - local_mean) * valid[:, None], axis=0)
    stats = jnp.stack([jnp.broadcast_to(count_local, local_sum.shape), local_mean, local_m2])
    stats = moments_over(stats, "tm")
    count, mean, m2 = stats[0], stats[1], stats[2]
    centred = conv - mean
    var = m2 / count
    scaled = centred * lax.rsqrt(var + 1e-05) * batch_gain + batch_bias
    swished = (scaled * jax.nn.sigmoid(scaled)).astype(jnp.bfloat16)
    swished_all = lax.all_gather(swished, "tensor", axis=1, tiled=True)
    swap = [(i, i ^ 1) for i in range(lax.axis_size("tm"))]
    out_other, ff_other = lax.ppermute(jnp.stack([out_mine, ff_mine]), "tm", swap)
    up_whole = jnp.where(my_core == 0, ff_mine, ff_other)
    down_t = jnp.where(my_core == 0, ff_other, ff_mine)
    left = jnp.where(my_core == 0, out_mine, out_other)
    right = jnp.where(my_core == 0, out_other, out_mine)
    contract = (((1,), (0,)), ((), ()))
    conv_out = jnp.concatenate(
        [
            lax.dot_general(swished_all, left, contract, preferred_element_type=jnp.float32),
            lax.dot_general(swished_all, right, contract, preferred_element_type=jnp.float32),
        ],
        axis=1,
    )
    mid_block = (feature_block.astype(jnp.float32) + conv_out).astype(jnp.bfloat16)
    mid_block, up_whole, down_t = lax.optimization_barrier((mid_block, up_whole, down_t))
    feed_block = layer_norm(mid_block, feed_gain).astype(jnp.bfloat16)
    mid = lax.dynamic_slice_in_dim(mid_block, lax.axis_index("tensor") * own_rows, own_rows, axis=0)
    pre = jnp.dot(feed_block, up_whole, preferred_element_type=jnp.float32)
    hidden = (pre * jax.nn.sigmoid(pre)).astype(jnp.bfloat16)
    partial_out = lax.dot_general(
        hidden, down_t, (((1,), (1,)), ((), ())), preferred_element_type=jnp.float32
    )
    feed_out = lax.psum_scatter(
        partial_out.astype(jnp.bfloat16), "tensor", scatter_dimension=0, tiled=True
    ).astype(jnp.float32)
    return (mid.astype(jnp.float32) + 0.5 * feed_out).astype(jnp.bfloat16)


def solution(mesh):
    placed = (
        P(("tm", "tensor"), None),
        P("tm"),
        P(),
        P(),
        P(None, "tensor"),
        P(None, "tensor"),
        P(None, "tensor"),
        P("tensor"),
        P("tensor"),
        P("tensor", None),
        P(),
        P("tm", "tensor"),
        P("tensor", "tm"),
    )
    return jax.shard_map(
        shards, mesh=mesh, in_specs=placed, out_specs=P(("tm", "tensor"), None), check_vma=False
    )
```

```python
import jax
import jax.numpy as jnp
from jax import lax
from jax.experimental.layout import Layout, with_layout_constraint
from jax.sharding import PartitionSpec as P

KERNEL = 31


def extended(array, sides, width):
    for axis, dim in sides:
        devices, length = (lax.axis_size(axis), array.shape[dim])
        up = [(i, (i + 1) % devices) for i in range(devices - 1)]
        down = [(j, i) for i, j in up]
        last = lax.slice_in_dim(array, length - width, length, axis=dim)
        initial = lax.slice_in_dim(array, 0, width, axis=dim)
        before = lax.ppermute(last, axis, up)
        after = lax.ppermute(initial, axis, down)
        array = jnp.concatenate([before, array, after], axis=dim)
    return array


def layer_norm(rows, gain):
    values = rows.astype(jnp.float32)
    centre = jnp.mean(values, axis=-1, keepdims=True)
    spread = jnp.mean(jnp.square(values - centre), axis=-1, keepdims=True)
    return (values - centre) * lax.rsqrt(spread + 1e-05) * gain


def merge_moments(low, high):
    n_a, mean_a, m2_a = low[0], low[1], low[2]
    n_b, mean_b, m2_b = high[0], high[1], high[2]
    n = n_a + n_b
    share = jnp.where(n > 0, n_b / jnp.maximum(n, 1.0), 0.0)
    delta = mean_b - mean_a
    mean = mean_a + delta * share
    m2 = m2_a + m2_b + jnp.square(delta) * n_a * share
    return jnp.stack([n, mean, m2])


def moments_over(stats, axis):
    size = lax.axis_size(axis)
    me = lax.axis_index(axis)
    step = 1
    while step < size:
        pairs = [(i, i ^ step) for i in range(size)]
        other = lax.ppermute(stats, axis, pairs)
        mine_low = (me & step) == 0
        low = jnp.where(mine_low, stats, other)
        high = jnp.where(mine_low, other, stats)
        stats = merge_moments(low, high)
        step *= 2
    return stats


def gather_torus(up_piece, down_piece, axis, tie):
    size = lax.axis_size(axis)
    cores, xs = 2, 4
    ys = size // (cores * xs)

    def coords(i):
        return i // (cores * xs), (i // cores) % xs, i % cores

    def index(y, x, c):
        return (y * xs + x) * cores + c

    me = lax.axis_index(axis)
    my_c = me % cores
    my_x = (me // cores) % xs
    my_y = me // (cores * xs)

    def shifted(value, move):
        pairs = []
        for i in range(size):
            y, x, c = coords(i)
            pairs.append((i, index(*move(y, x, c))))
        return lax.ppermute(value, axis, pairs)

    def ordered(own, received, mine, count):
        slots = [own] + received
        picks = []
        for j in range(count):
            k = (mine - j) % count
            picked = slots[0]
            for t in range(1, count):
                picked = jnp.where(k == t, slots[t], picked)
            picks.append(picked)
        return picks

    partner = lambda y, x, c: (y, x, 1 - c)
    other_up, other_down = shifted((up_piece, down_piece), partner)
    pair_up = jnp.concatenate(ordered(up_piece, [other_up], my_c, cores), axis=0)
    pair_down = jnp.concatenate(ordered(down_piece, [other_down], my_c, cores), axis=0)
    pair = jnp.where(my_c == 0, pair_up, pair_down)
    got = [shifted(pair, lambda y, x, c, d=d: (y, (x + d) % xs, c)) for d in range(1, xs)]
    row = jnp.concatenate(ordered(pair, got, my_x, xs), axis=0)
    got = [shifted(row, lambda y, x, c, d=d: ((y + d) % ys, x, c)) for d in range(1, ys)]
    whole = jnp.concatenate(ordered(row, got, my_y, ys), axis=0)
    whole, tie = lax.optimization_barrier((whole, tie))
    swapped = shifted(whole, partner)
    up_whole = jnp.where(my_c == 0, whole, swapped)
    down_whole = jnp.where(my_c == 0, swapped, whole)
    return up_whole, down_whole, tie


def shards(
    features,
    frame_mask,
    total_length,
    norm_gain,
    value_weight,
    gate_weight,
    depth_kernel,
    batch_gain,
    batch_bias,
    out_weight,
    feed_gain,
    up_weight,
    down_weight,
):
    own_rows = features.shape[0]
    block = own_rows * lax.axis_size("tensor")
    positions = lax.axis_index("tm") * block + jnp.arange(block, dtype=jnp.int32)
    valid = ((frame_mask > 0) & (positions < total_length[0])).astype(jnp.float32)
    feature_block = lax.all_gather(features, "tensor", axis=0, tiled=True)
    feature_block = with_layout_constraint(feature_block, Layout(major_to_minor=(0, 1)))
    piece = layer_norm(feature_block, norm_gain).astype(jnp.bfloat16)
    my_core = lax.axis_index("tm") % 2
    cols = out_weight.shape[1] // 2
    out_half = jnp.where(my_core == 0, out_weight[:, :cols], out_weight[:, cols:])
    out_mine = lax.all_gather(out_half, "tensor", axis=0, tiled=True)
    value = jnp.dot(piece, value_weight, preferred_element_type=jnp.float32)
    gate = jnp.dot(piece, gate_weight, preferred_element_type=jnp.float32)
    glu = (value * jax.nn.sigmoid(gate) * valid[:, None]).astype(jnp.bfloat16)
    up_whole, down_t, glu = gather_torus(up_weight, down_weight.T, "tm", glu)
    reach = KERNEL // 2
    edges = jnp.concatenate([piece[:reach], piece[block - reach :]], axis=0)
    edge_valid = jnp.concatenate([valid[:reach], valid[block - reach :]], axis=0)
    edge_value = jnp.dot(edges, value_weight, preferred_element_type=jnp.float32)
    edge_gate = jnp.dot(edges, gate_weight, preferred_element_type=jnp.float32)
    edge_glu = (edge_value * jax.nn.sigmoid(edge_gate) * edge_valid[:, None]).astype(jnp.bfloat16)
    devices = lax.axis_size("tm")
    up = [(i, (i + 1) % devices) for i in range(devices - 1)]
    down = [(j, i) for i, j in up]
    before = lax.ppermute(edge_glu[reach:], "tm", up)
    after = lax.ppermute(edge_glu[:reach], "tm", down)
    padded = jnp.concatenate([before, glu, after], axis=0)
    conv = jnp.zeros(glu.shape, jnp.float32)
    for tap in range(KERNEL):
        conv = conv + padded[tap : tap + block].astype(jnp.float32) * depth_kernel[tap]
    count_local = jnp.sum(valid)
    local_sum = jnp.sum(conv * valid[:, None], axis=0)
    local_mean = jnp.where(count_local > 0, local_sum / jnp.maximum(count_local, 1.0), 0.0)
    local_m2 = jnp.sum(jnp.square(conv - local_mean) * valid[:, None], axis=0)
    stats = jnp.stack([jnp.broadcast_to(count_local, local_sum.shape), local_mean, local_m2])
    stats = moments_over(stats, "tm")
    count, mean, m2 = stats[0], stats[1], stats[2]
    centred = conv - mean
    var = m2 / count
    scaled = centred * lax.rsqrt(var + 1e-05) * batch_gain + batch_bias
    swished = (scaled * jax.nn.sigmoid(scaled)).astype(jnp.bfloat16)
    swished_all = lax.all_gather(swished, "tensor", axis=1, tiled=True)
    out_other = lax.ppermute(out_mine, "tm", [(i, i ^ 1) for i in range(lax.axis_size("tm"))])
    left = jnp.where(my_core == 0, out_mine, out_other)
    right = jnp.where(my_core == 0, out_other, out_mine)
    contract = (((1,), (0,)), ((), ()))
    conv_out = jnp.concatenate(
        [
            lax.dot_general(swished_all, left, contract, preferred_element_type=jnp.float32),
            lax.dot_general(swished_all, right, contract, preferred_element_type=jnp.float32),
        ],
        axis=1,
    )
    mid_block = (feature_block.astype(jnp.float32) + conv_out).astype(jnp.bfloat16)
    mid_block, up_whole, down_t = lax.optimization_barrier((mid_block, up_whole, down_t))
    feed_block = layer_norm(mid_block, feed_gain).astype(jnp.bfloat16)
    mid = lax.dynamic_slice_in_dim(mid_block, lax.axis_index("tensor") * own_rows, own_rows, axis=0)
    pre = jnp.dot(feed_block, up_whole, preferred_element_type=jnp.float32)
    hidden = (pre * jax.nn.sigmoid(pre)).astype(jnp.bfloat16)
    partial_out = lax.dot_general(
        hidden, down_t, (((1,), (1,)), ((), ())), preferred_element_type=jnp.float32
    )
    feed_out = lax.psum_scatter(
        partial_out.astype(jnp.bfloat16), "tensor", scatter_dimension=0, tiled=True
    ).astype(jnp.float32)
    return (mid.astype(jnp.float32) + 0.5 * feed_out).astype(jnp.bfloat16)


def solution(mesh):
    placed = (
        P(("tm", "tensor"), None),
        P("tm"),
        P(),
        P(),
        P(None, "tensor"),
        P(None, "tensor"),
        P(None, "tensor"),
        P("tensor"),
        P("tensor"),
        P("tensor", None),
        P(),
        P("tm", "tensor"),
        P("tensor", "tm"),
    )
    return jax.shard_map(
        shards, mesh=mesh, in_specs=placed, out_specs=P(("tm", "tensor"), None), check_vma=False
    )
```

```python
import jax
import jax.numpy as jnp
from jax import lax
from jax.experimental.layout import Layout, with_layout_constraint
from jax.sharding import PartitionSpec as P

KERNEL = 31


def extended(array, sides, width):
    for axis, dim in sides:
        devices, length = (lax.axis_size(axis), array.shape[dim])
        up = [(i, (i + 1) % devices) for i in range(devices - 1)]
        down = [(j, i) for i, j in up]
        last = lax.slice_in_dim(array, length - width, length, axis=dim)
        initial = lax.slice_in_dim(array, 0, width, axis=dim)
        before = lax.ppermute(last, axis, up)
        after = lax.ppermute(initial, axis, down)
        array = jnp.concatenate([before, array, after], axis=dim)
    return array


def layer_norm(rows, gain):
    values = rows.astype(jnp.float32)
    centre = jnp.mean(values, axis=-1, keepdims=True)
    spread = jnp.mean(jnp.square(values - centre), axis=-1, keepdims=True)
    return (values - centre) * lax.rsqrt(spread + 1e-05) * gain


def merge_moments(low, high):
    n_a, mean_a, m2_a = low[0], low[1], low[2]
    n_b, mean_b, m2_b = high[0], high[1], high[2]
    n = n_a + n_b
    share = jnp.where(n > 0, n_b / jnp.maximum(n, 1.0), 0.0)
    delta = mean_b - mean_a
    mean = mean_a + delta * share
    m2 = m2_a + m2_b + jnp.square(delta) * n_a * share
    return jnp.stack([n, mean, m2])


def moments_over(stats, axis):
    size = lax.axis_size(axis)
    me = lax.axis_index(axis)
    step = 1
    while step < size:
        pairs = [(i, i ^ step) for i in range(size)]
        other = lax.ppermute(stats, axis, pairs)
        mine_low = (me & step) == 0
        low = jnp.where(mine_low, stats, other)
        high = jnp.where(mine_low, other, stats)
        stats = merge_moments(low, high)
        step *= 2
    return stats


def gather_torus(up_piece, down_piece, axis, tie):
    size = lax.axis_size(axis)
    cores, xs = 2, 4
    ys = size // (cores * xs)

    def coords(i):
        return i // (cores * xs), (i // cores) % xs, i % cores

    def index(y, x, c):
        return (y * xs + x) * cores + c

    me = lax.axis_index(axis)
    my_c = me % cores
    my_x = (me // cores) % xs
    my_y = me // (cores * xs)

    def shifted(value, move):
        pairs = []
        for i in range(size):
            y, x, c = coords(i)
            pairs.append((i, index(*move(y, x, c))))
        return lax.ppermute(value, axis, pairs)

    def ordered(own, received, mine, count):
        slots = [own] + received
        picks = []
        for j in range(count):
            k = (mine - j) % count
            picked = slots[0]
            for t in range(1, count):
                picked = jnp.where(k == t, slots[t], picked)
            picks.append(picked)
        return picks

    partner = lambda y, x, c: (y, x, 1 - c)
    other = shifted(jnp.stack([up_piece, down_piece]), partner)
    other_up, other_down = other[0], other[1]
    pair_up = jnp.concatenate(ordered(up_piece, [other_up], my_c, cores), axis=0)
    pair_down = jnp.concatenate(ordered(down_piece, [other_down], my_c, cores), axis=0)
    pair = jnp.where(my_c == 0, pair_up, pair_down)
    got = [shifted(pair, lambda y, x, c, d=d: (y, (x + d) % xs, c)) for d in range(1, xs)]
    row = jnp.concatenate(ordered(pair, got, my_x, xs), axis=0)
    got = [shifted(row, lambda y, x, c, d=d: ((y + d) % ys, x, c)) for d in range(1, ys)]
    whole = jnp.concatenate(ordered(row, got, my_y, ys), axis=0)
    whole, tie = lax.optimization_barrier((whole, tie))
    return whole, tie


def shards(
    features,
    frame_mask,
    total_length,
    norm_gain,
    value_weight,
    gate_weight,
    depth_kernel,
    batch_gain,
    batch_bias,
    out_weight,
    feed_gain,
    up_weight,
    down_weight,
):
    own_rows = features.shape[0]
    block = own_rows * lax.axis_size("tensor")
    positions = lax.axis_index("tm") * block + jnp.arange(block, dtype=jnp.int32)
    valid = ((frame_mask > 0) & (positions < total_length[0])).astype(jnp.float32)
    feature_block = lax.all_gather(features, "tensor", axis=0, tiled=True)
    feature_block = with_layout_constraint(feature_block, Layout(major_to_minor=(0, 1)))
    piece = layer_norm(feature_block, norm_gain).astype(jnp.bfloat16)
    my_core = lax.axis_index("tm") % 2
    cols = out_weight.shape[1] // 2
    out_half = jnp.where(my_core == 0, out_weight[:, :cols], out_weight[:, cols:])
    out_mine = lax.all_gather(out_half, "tensor", axis=0, tiled=True)
    value = jnp.dot(piece, value_weight, preferred_element_type=jnp.float32)
    gate = jnp.dot(piece, gate_weight, preferred_element_type=jnp.float32)
    glu = (value * jax.nn.sigmoid(gate) * valid[:, None]).astype(jnp.bfloat16)
    ff_mine, glu = gather_torus(up_weight, down_weight.T, "tm", glu)
    padded = extended(glu, (("tm", 0),), KERNEL // 2)
    conv = jnp.zeros(glu.shape, jnp.float32)
    for tap in range(KERNEL):
        conv = conv + padded[tap : tap + block].astype(jnp.float32) * depth_kernel[tap]
    count_local = jnp.sum(valid)
    local_sum = jnp.sum(conv * valid[:, None], axis=0)
    local_mean = jnp.where(count_local > 0, local_sum / jnp.maximum(count_local, 1.0), 0.0)
    local_m2 = jnp.sum(jnp.square(conv - local_mean) * valid[:, None], axis=0)
    stats = jnp.stack([jnp.broadcast_to(count_local, local_sum.shape), local_mean, local_m2])
    stats = moments_over(stats, "tm")
    count, mean, m2 = stats[0], stats[1], stats[2]
    centred = conv - mean
    var = m2 / count
    scaled = centred * lax.rsqrt(var + 1e-05) * batch_gain + batch_bias
    swished = (scaled * jax.nn.sigmoid(scaled)).astype(jnp.bfloat16)
    swished_all = lax.all_gather(swished, "tensor", axis=1, tiled=True)
    swap = [(i, i ^ 1) for i in range(lax.axis_size("tm"))]
    out_other, ff_other = lax.ppermute(jnp.stack([out_mine, ff_mine]), "tm", swap)
    up_whole = jnp.where(my_core == 0, ff_mine, ff_other)
    down_t = jnp.where(my_core == 0, ff_other, ff_mine)
    left = jnp.where(my_core == 0, out_mine, out_other)
    right = jnp.where(my_core == 0, out_other, out_mine)
    contract = (((1,), (0,)), ((), ()))
    conv_out = jnp.concatenate(
        [
            lax.dot_general(swished_all, left, contract, preferred_element_type=jnp.float32),
            lax.dot_general(swished_all, right, contract, preferred_element_type=jnp.float32),
        ],
        axis=1,
    )
    mid_block = (feature_block.astype(jnp.float32) + conv_out).astype(jnp.bfloat16)
    mid_block, up_whole, down_t = lax.optimization_barrier((mid_block, up_whole, down_t))
    feed_block = layer_norm(mid_block, feed_gain).astype(jnp.bfloat16)
    mid = lax.dynamic_slice_in_dim(mid_block, lax.axis_index("tensor") * own_rows, own_rows, axis=0)
    pre = jnp.dot(feed_block, up_whole, preferred_element_type=jnp.float32)
    hidden = (pre * jax.nn.sigmoid(pre)).astype(jnp.bfloat16)
    partial_out = lax.dot_general(
        hidden, down_t, (((1,), (1,)), ((), ())), preferred_element_type=jnp.float32
    )
    feed_out = lax.psum_scatter(
        partial_out.astype(jnp.bfloat16), "tensor", scatter_dimension=0, tiled=True
    ).astype(jnp.float32)
    return (mid.astype(jnp.float32) + 0.5 * feed_out).astype(jnp.bfloat16)


def solution(mesh):
    placed = (
        P(("tm", "tensor"), None),
        P("tm"),
        P(),
        P(),
        P(None, "tensor"),
        P(None, "tensor"),
        P(None, "tensor"),
        P("tensor"),
        P("tensor"),
        P("tensor", None),
        P(),
        P("tm", "tensor"),
        P("tensor", "tm"),
    )
    return jax.shard_map(
        shards, mesh=mesh, in_specs=placed, out_specs=P(("tm", "tensor"), None), check_vma=False
    )
```

```python
import jax
import jax.numpy as jnp
from jax import lax
from jax.experimental.layout import Layout, with_layout_constraint
from jax.sharding import PartitionSpec as P

KERNEL = 31


def extended(array, sides, width):
    for axis, dim in sides:
        devices, length = (lax.axis_size(axis), array.shape[dim])
        up = [(i, (i + 1) % devices) for i in range(devices - 1)]
        down = [(j, i) for i, j in up]
        last = lax.slice_in_dim(array, length - width, length, axis=dim)
        initial = lax.slice_in_dim(array, 0, width, axis=dim)
        before = lax.ppermute(last, axis, up)
        after = lax.ppermute(initial, axis, down)
        array = jnp.concatenate([before, array, after], axis=dim)
    return array


def layer_norm(rows, gain):
    values = rows.astype(jnp.float32)
    centre = jnp.mean(values, axis=-1, keepdims=True)
    spread = jnp.mean(jnp.square(values - centre), axis=-1, keepdims=True)
    return (values - centre) * lax.rsqrt(spread + 1e-05) * gain


def merge_moments(low, high):
    n_a, mean_a, m2_a = low[0], low[1], low[2]
    n_b, mean_b, m2_b = high[0], high[1], high[2]
    n = n_a + n_b
    share = jnp.where(n > 0, n_b / jnp.maximum(n, 1.0), 0.0)
    delta = mean_b - mean_a
    mean = mean_a + delta * share
    m2 = m2_a + m2_b + jnp.square(delta) * n_a * share
    return jnp.stack([n, mean, m2])


def moments_over(stats, axis):
    size = lax.axis_size(axis)
    me = lax.axis_index(axis)
    step = 1
    while step < size:
        pairs = [(i, i ^ step) for i in range(size)]
        other = lax.ppermute(stats, axis, pairs)
        mine_low = (me & step) == 0
        low = jnp.where(mine_low, stats, other)
        high = jnp.where(mine_low, other, stats)
        stats = merge_moments(low, high)
        step *= 2
    return stats


def gather_torus(up_piece, down_piece, axis, tie):
    size = lax.axis_size(axis)
    cores, xs = 2, 4
    ys = size // (cores * xs)

    def coords(i):
        return i // (cores * xs), (i // cores) % xs, i % cores

    def index(y, x, c):
        return (y * xs + x) * cores + c

    me = lax.axis_index(axis)
    my_c = me % cores
    my_x = (me // cores) % xs
    my_y = me // (cores * xs)

    def shifted(value, move):
        pairs = []
        for i in range(size):
            y, x, c = coords(i)
            pairs.append((i, index(*move(y, x, c))))
        return lax.ppermute(value, axis, pairs)

    def ordered(own, received, mine, count):
        slots = [own] + received
        picks = []
        for j in range(count):
            k = (mine - j) % count
            picked = slots[0]
            for t in range(1, count):
                picked = jnp.where(k == t, slots[t], picked)
            picks.append(picked)
        return picks

    partner = lambda y, x, c: (y, x, 1 - c)
    other = shifted(jnp.stack([up_piece, down_piece]), partner)
    other_up, other_down = other[0], other[1]
    pair_up = jnp.concatenate(ordered(up_piece, [other_up], my_c, cores), axis=0)
    pair_down = jnp.concatenate(ordered(down_piece, [other_down], my_c, cores), axis=0)
    pair = jnp.where(my_c == 0, pair_up, pair_down)
    def doubled(value, mine, count, move):
        step = 1
        while step < count:
            other = shifted(value, lambda y, x, c, s=step: move(y, x, c, s))
            low = (mine & step) == 0
            value = jnp.where(
                low,
                jnp.concatenate([value, other], axis=0),
                jnp.concatenate([other, value], axis=0),
            )
            step *= 2
        return value

    row = doubled(pair, my_x, xs, lambda y, x, c, s: (y, x ^ s, c))
    whole = doubled(row, my_y, ys, lambda y, x, c, s: (y ^ s, x, c))
    whole, tie = lax.optimization_barrier((whole, tie))
    return whole, tie


def shards(
    features,
    frame_mask,
    total_length,
    norm_gain,
    value_weight,
    gate_weight,
    depth_kernel,
    batch_gain,
    batch_bias,
    out_weight,
    feed_gain,
    up_weight,
    down_weight,
):
    own_rows = features.shape[0]
    block = own_rows * lax.axis_size("tensor")
    positions = lax.axis_index("tm") * block + jnp.arange(block, dtype=jnp.int32)
    valid = ((frame_mask > 0) & (positions < total_length[0])).astype(jnp.float32)
    feature_block = lax.all_gather(features, "tensor", axis=0, tiled=True)
    feature_block = with_layout_constraint(feature_block, Layout(major_to_minor=(0, 1)))
    piece = layer_norm(feature_block, norm_gain).astype(jnp.bfloat16)
    my_core = lax.axis_index("tm") % 2
    cols = out_weight.shape[1] // 2
    out_half = jnp.where(my_core == 0, out_weight[:, :cols], out_weight[:, cols:])
    out_mine = lax.all_gather(out_half, "tensor", axis=0, tiled=True)
    value = jnp.dot(piece, value_weight, preferred_element_type=jnp.float32)
    gate = jnp.dot(piece, gate_weight, preferred_element_type=jnp.float32)
    glu = (value * jax.nn.sigmoid(gate) * valid[:, None]).astype(jnp.bfloat16)
    ff_mine, glu = gather_torus(up_weight, down_weight.T, "tm", glu)
    padded = extended(glu, (("tm", 0),), KERNEL // 2)
    conv = jnp.zeros(glu.shape, jnp.float32)
    for tap in range(KERNEL):
        conv = conv + padded[tap : tap + block].astype(jnp.float32) * depth_kernel[tap]
    count_local = jnp.sum(valid)
    local_sum = jnp.sum(conv * valid[:, None], axis=0)
    local_mean = jnp.where(count_local > 0, local_sum / jnp.maximum(count_local, 1.0), 0.0)
    local_m2 = jnp.sum(jnp.square(conv - local_mean) * valid[:, None], axis=0)
    stats = jnp.stack([jnp.broadcast_to(count_local, local_sum.shape), local_mean, local_m2])
    stats = moments_over(stats, "tm")
    count, mean, m2 = stats[0], stats[1], stats[2]
    centred = conv - mean
    var = m2 / count
    scaled = centred * lax.rsqrt(var + 1e-05) * batch_gain + batch_bias
    swished = (scaled * jax.nn.sigmoid(scaled)).astype(jnp.bfloat16)
    swished_all = lax.all_gather(swished, "tensor", axis=1, tiled=True)
    swap = [(i, i ^ 1) for i in range(lax.axis_size("tm"))]
    out_other, ff_other = lax.ppermute(jnp.stack([out_mine, ff_mine]), "tm", swap)
    up_whole = jnp.where(my_core == 0, ff_mine, ff_other)
    down_t = jnp.where(my_core == 0, ff_other, ff_mine)
    left = jnp.where(my_core == 0, out_mine, out_other)
    right = jnp.where(my_core == 0, out_other, out_mine)
    contract = (((1,), (0,)), ((), ()))
    conv_out = jnp.concatenate(
        [
            lax.dot_general(swished_all, left, contract, preferred_element_type=jnp.float32),
            lax.dot_general(swished_all, right, contract, preferred_element_type=jnp.float32),
        ],
        axis=1,
    )
    mid_block = (feature_block.astype(jnp.float32) + conv_out).astype(jnp.bfloat16)
    mid_block, up_whole, down_t = lax.optimization_barrier((mid_block, up_whole, down_t))
    feed_block = layer_norm(mid_block, feed_gain).astype(jnp.bfloat16)
    mid = lax.dynamic_slice_in_dim(mid_block, lax.axis_index("tensor") * own_rows, own_rows, axis=0)
    pre = jnp.dot(feed_block, up_whole, preferred_element_type=jnp.float32)
    hidden = (pre * jax.nn.sigmoid(pre)).astype(jnp.bfloat16)
    partial_out = lax.dot_general(
        hidden, down_t, (((1,), (1,)), ((), ())), preferred_element_type=jnp.float32
    )
    feed_out = lax.psum_scatter(
        partial_out.astype(jnp.bfloat16), "tensor", scatter_dimension=0, tiled=True
    ).astype(jnp.float32)
    return (mid.astype(jnp.float32) + 0.5 * feed_out).astype(jnp.bfloat16)


def solution(mesh):
    placed = (
        P(("tm", "tensor"), None),
        P("tm"),
        P(),
        P(),
        P(None, "tensor"),
        P(None, "tensor"),
        P(None, "tensor"),
        P("tensor"),
        P("tensor"),
        P("tensor", None),
        P(),
        P("tm", "tensor"),
        P("tensor", "tm"),
    )
    return jax.shard_map(
        shards, mesh=mesh, in_specs=placed, out_specs=P(("tm", "tensor"), None), check_vma=False
    )
```

```python
import jax
import jax.numpy as jnp
from jax import lax
from jax.experimental.layout import Layout, with_layout_constraint
from jax.sharding import PartitionSpec as P

KERNEL = 31


def extended(array, sides, width):
    for axis, dim in sides:
        devices, length = (lax.axis_size(axis), array.shape[dim])
        up = [(i, (i + 1) % devices) for i in range(devices - 1)]
        down = [(j, i) for i, j in up]
        last = lax.slice_in_dim(array, length - width, length, axis=dim)
        initial = lax.slice_in_dim(array, 0, width, axis=dim)
        before = lax.ppermute(last, axis, up)
        after = lax.ppermute(initial, axis, down)
        array = jnp.concatenate([before, array, after], axis=dim)
    return array


def layer_norm(rows, gain):
    values = rows.astype(jnp.float32)
    centre = jnp.mean(values, axis=-1, keepdims=True)
    spread = jnp.mean(jnp.square(values - centre), axis=-1, keepdims=True)
    return (values - centre) * lax.rsqrt(spread + 1e-05) * gain


def merge_moments(low, high):
    n_a, mean_a, m2_a = low[0], low[1], low[2]
    n_b, mean_b, m2_b = high[0], high[1], high[2]
    n = n_a + n_b
    share = jnp.where(n > 0, n_b / jnp.maximum(n, 1.0), 0.0)
    delta = mean_b - mean_a
    mean = mean_a + delta * share
    m2 = m2_a + m2_b + jnp.square(delta) * n_a * share
    return jnp.stack([n, mean, m2])


def moments_over(stats, axis):
    size = lax.axis_size(axis)
    me = lax.axis_index(axis)
    step = 1
    while step < size:
        pairs = [(i, i ^ step) for i in range(size)]
        other = lax.ppermute(stats, axis, pairs)
        mine_low = (me & step) == 0
        low = jnp.where(mine_low, stats, other)
        high = jnp.where(mine_low, other, stats)
        stats = merge_moments(low, high)
        step *= 2
    return stats


def gather_torus(up_piece, down_piece, axis, tie):
    size = lax.axis_size(axis)
    cores, xs = 2, 4
    ys = size // (cores * xs)

    def coords(i):
        return i // (cores * xs), (i // cores) % xs, i % cores

    def index(y, x, c):
        return (y * xs + x) * cores + c

    me = lax.axis_index(axis)
    my_c = me % cores
    my_x = (me // cores) % xs
    my_y = me // (cores * xs)

    def shifted(value, move):
        pairs = []
        for i in range(size):
            y, x, c = coords(i)
            pairs.append((i, index(*move(y, x, c))))
        return lax.ppermute(value, axis, pairs)

    def ordered(own, received, mine, count):
        slots = [own] + received
        picks = []
        for j in range(count):
            k = (mine - j) % count
            picked = slots[0]
            for t in range(1, count):
                picked = jnp.where(k == t, slots[t], picked)
            picks.append(picked)
        return picks

    partner = lambda y, x, c: (y, x, 1 - c)
    other = shifted(jnp.stack([up_piece, down_piece]), partner)
    other_up, other_down = other[0], other[1]
    pair_up = jnp.concatenate(ordered(up_piece, [other_up], my_c, cores), axis=0)
    pair_down = jnp.concatenate(ordered(down_piece, [other_down], my_c, cores), axis=0)
    pair = jnp.where(my_c == 0, pair_up, pair_down)
    got = [shifted(pair, lambda y, x, c, d=d: (y, (x + d) % xs, c)) for d in range(1, xs)]
    row = jnp.concatenate(ordered(pair, got, my_x, xs), axis=0)
    got = [shifted(row, lambda y, x, c, d=d: ((y + d) % ys, x, c)) for d in range(1, ys)]
    whole = jnp.concatenate(ordered(row, got, my_y, ys), axis=0)
    whole, tie = lax.optimization_barrier((whole, tie))
    return whole, tie


def gather_tensor(values, axis):
    size = lax.axis_size(axis)
    me = lax.axis_index(axis)
    step = 1
    while step < size:
        other = lax.ppermute(values, axis, [(i, i ^ step) for i in range(size)])
        mine_low = (me & step) == 0
        values = jnp.where(
            mine_low,
            jnp.concatenate([values, other], axis=-1),
            jnp.concatenate([other, values], axis=-1),
        )
        step *= 2
    return values


def shards(
    features,
    frame_mask,
    total_length,
    norm_gain,
    value_weight,
    gate_weight,
    depth_kernel,
    batch_gain,
    batch_bias,
    out_weight,
    feed_gain,
    up_weight,
    down_weight,
):
    own_rows = features.shape[0]
    block = own_rows * lax.axis_size("tensor")
    positions = lax.axis_index("tm") * block + jnp.arange(block, dtype=jnp.int32)
    valid = ((frame_mask > 0) & (positions < total_length[0])).astype(jnp.float32)
    feature_block = lax.all_gather(features, "tensor", axis=0, tiled=True)
    feature_block = with_layout_constraint(feature_block, Layout(major_to_minor=(0, 1)))
    own = features.astype(jnp.float32)
    centre = jnp.mean(own, axis=-1)
    spread = jnp.mean(jnp.square(own - centre[:, None]), axis=-1)
    rows = gather_tensor(jnp.stack([centre, lax.rsqrt(spread + 1e-05)]), "tensor")
    piece = (
        (feature_block.astype(jnp.float32) - rows[0][:, None]) * rows[1][:, None] * norm_gain
    ).astype(jnp.bfloat16)
    my_core = lax.axis_index("tm") % 2
    cols = out_weight.shape[1] // 2
    out_half = jnp.where(my_core == 0, out_weight[:, :cols], out_weight[:, cols:])
    out_mine = lax.all_gather(out_half, "tensor", axis=0, tiled=True)
    value = jnp.dot(piece, value_weight, preferred_element_type=jnp.float32)
    gate = jnp.dot(piece, gate_weight, preferred_element_type=jnp.float32)
    glu = (value * jax.nn.sigmoid(gate) * valid[:, None]).astype(jnp.bfloat16)
    ff_mine, glu = gather_torus(up_weight, down_weight.T, "tm", glu)
    padded = extended(glu, (("tm", 0),), KERNEL // 2)
    conv = jnp.zeros(glu.shape, jnp.float32)
    for tap in range(KERNEL):
        conv = conv + padded[tap : tap + block].astype(jnp.float32) * depth_kernel[tap]
    count_local = jnp.sum(valid)
    local_sum = jnp.sum(conv * valid[:, None], axis=0)
    local_mean = jnp.where(count_local > 0, local_sum / jnp.maximum(count_local, 1.0), 0.0)
    local_m2 = jnp.sum(jnp.square(conv - local_mean) * valid[:, None], axis=0)
    stats = jnp.stack([jnp.broadcast_to(count_local, local_sum.shape), local_mean, local_m2])
    stats = moments_over(stats, "tm")
    count, mean, m2 = stats[0], stats[1], stats[2]
    centred = conv - mean
    var = m2 / count
    scaled = centred * lax.rsqrt(var + 1e-05) * batch_gain + batch_bias
    swished = (scaled * jax.nn.sigmoid(scaled)).astype(jnp.bfloat16)
    swished_all = lax.all_gather(swished, "tensor", axis=1, tiled=True)
    swap = [(i, i ^ 1) for i in range(lax.axis_size("tm"))]
    out_other, ff_other = lax.ppermute(jnp.stack([out_mine, ff_mine]), "tm", swap)
    up_whole = jnp.where(my_core == 0, ff_mine, ff_other)
    down_t = jnp.where(my_core == 0, ff_other, ff_mine)
    left = jnp.where(my_core == 0, out_mine, out_other)
    right = jnp.where(my_core == 0, out_other, out_mine)
    contract = (((1,), (0,)), ((), ()))
    conv_out = jnp.concatenate(
        [
            lax.dot_general(swished_all, left, contract, preferred_element_type=jnp.float32),
            lax.dot_general(swished_all, right, contract, preferred_element_type=jnp.float32),
        ],
        axis=1,
    )
    mid_block = (feature_block.astype(jnp.float32) + conv_out).astype(jnp.bfloat16)
    mid_block, up_whole, down_t = lax.optimization_barrier((mid_block, up_whole, down_t))
    feed_block = layer_norm(mid_block, feed_gain).astype(jnp.bfloat16)
    mid = lax.dynamic_slice_in_dim(mid_block, lax.axis_index("tensor") * own_rows, own_rows, axis=0)
    pre = jnp.dot(feed_block, up_whole, preferred_element_type=jnp.float32)
    hidden = (pre * jax.nn.sigmoid(pre)).astype(jnp.bfloat16)
    partial_out = lax.dot_general(
        hidden, down_t, (((1,), (1,)), ((), ())), preferred_element_type=jnp.float32
    )
    feed_out = lax.psum_scatter(
        partial_out.astype(jnp.bfloat16), "tensor", scatter_dimension=0, tiled=True
    ).astype(jnp.float32)
    return (mid.astype(jnp.float32) + 0.5 * feed_out).astype(jnp.bfloat16)


def solution(mesh):
    placed = (
        P(("tm", "tensor"), None),
        P("tm"),
        P(),
        P(),
        P(None, "tensor"),
        P(None, "tensor"),
        P(None, "tensor"),
        P("tensor"),
        P("tensor"),
        P("tensor", None),
        P(),
        P("tm", "tensor"),
        P("tensor", "tm"),
    )
    return jax.shard_map(
        shards, mesh=mesh, in_specs=placed, out_specs=P(("tm", "tensor"), None), check_vma=False
    )
```

```python
import jax
import jax.numpy as jnp
from jax import lax
from jax.experimental.layout import Layout, with_layout_constraint
from jax.sharding import PartitionSpec as P

KERNEL = 31


def extended(array, sides, width):
    for axis, dim in sides:
        devices, length = (lax.axis_size(axis), array.shape[dim])
        up = [(i, (i + 1) % devices) for i in range(devices - 1)]
        down = [(j, i) for i, j in up]
        last = lax.slice_in_dim(array, length - width, length, axis=dim)
        initial = lax.slice_in_dim(array, 0, width, axis=dim)
        before = lax.ppermute(last, axis, up)
        after = lax.ppermute(initial, axis, down)
        array = jnp.concatenate([before, array, after], axis=dim)
    return array


def layer_norm(rows, gain):
    values = rows.astype(jnp.float32)
    centre = jnp.mean(values, axis=-1, keepdims=True)
    spread = jnp.mean(jnp.square(values - centre), axis=-1, keepdims=True)
    return (values - centre) * lax.rsqrt(spread + 1e-05) * gain


def merge_moments(low, high):
    n_a, mean_a, m2_a = low[0], low[1], low[2]
    n_b, mean_b, m2_b = high[0], high[1], high[2]
    n = n_a + n_b
    share = jnp.where(n > 0, n_b / jnp.maximum(n, 1.0), 0.0)
    delta = mean_b - mean_a
    mean = mean_a + delta * share
    m2 = m2_a + m2_b + jnp.square(delta) * n_a * share
    return jnp.stack([n, mean, m2])


def moments_over(stats, axis):
    size = lax.axis_size(axis)
    me = lax.axis_index(axis)
    step = 1
    while step < size:
        pairs = [(i, i ^ step) for i in range(size)]
        other = lax.ppermute(stats, axis, pairs)
        mine_low = (me & step) == 0
        low = jnp.where(mine_low, stats, other)
        high = jnp.where(mine_low, other, stats)
        stats = merge_moments(low, high)
        step *= 2
    return stats


def gather_torus(up_piece, down_piece, axis, tie):
    size = lax.axis_size(axis)
    cores, xs = 2, 4
    ys = size // (cores * xs)

    def coords(i):
        return i // (cores * xs), (i // cores) % xs, i % cores

    def index(y, x, c):
        return (y * xs + x) * cores + c

    me = lax.axis_index(axis)
    my_c = me % cores
    my_x = (me // cores) % xs
    my_y = me // (cores * xs)

    def shifted(value, move):
        pairs = []
        for i in range(size):
            y, x, c = coords(i)
            pairs.append((i, index(*move(y, x, c))))
        return lax.ppermute(value, axis, pairs)

    def ordered(own, received, mine, count):
        slots = [own] + received
        picks = []
        for j in range(count):
            k = (mine - j) % count
            picked = slots[0]
            for t in range(1, count):
                picked = jnp.where(k == t, slots[t], picked)
            picks.append(picked)
        return picks

    partner = lambda y, x, c: (y, x, 1 - c)
    other = shifted(jnp.stack([up_piece, down_piece]), partner)
    other_up, other_down = other[0], other[1]
    pair_up = jnp.concatenate(ordered(up_piece, [other_up], my_c, cores), axis=0)
    pair_down = jnp.concatenate(ordered(down_piece, [other_down], my_c, cores), axis=0)
    pair = jnp.where(my_c == 0, pair_up, pair_down)
    got = [shifted(pair, lambda y, x, c, d=d: (y, (x + d) % xs, c)) for d in range(1, xs)]
    row = jnp.concatenate(ordered(pair, got, my_x, xs), axis=0)
    got = [shifted(row, lambda y, x, c, d=d: ((y + d) % ys, x, c)) for d in range(1, ys)]
    whole = jnp.concatenate(ordered(row, got, my_y, ys), axis=0)
    whole, tie = lax.optimization_barrier((whole, tie))
    return whole, tie


def shards(
    features,
    frame_mask,
    total_length,
    norm_gain,
    value_weight,
    gate_weight,
    depth_kernel,
    batch_gain,
    batch_bias,
    out_weight,
    feed_gain,
    up_weight,
    down_weight,
):
    own_rows = features.shape[0]
    block = own_rows * lax.axis_size("tensor")
    positions = lax.axis_index("tm") * block + jnp.arange(block, dtype=jnp.int32)
    valid = ((frame_mask > 0) & (positions < total_length[0])).astype(jnp.float32)
    feature_block = lax.all_gather(features, "tensor", axis=0, tiled=True)
    feature_block = with_layout_constraint(feature_block, Layout(major_to_minor=(0, 1)))
    piece = layer_norm(feature_block, norm_gain).astype(jnp.bfloat16)
    my_core = lax.axis_index("tm") % 2
    cols = out_weight.shape[1] // 2
    out_half = jnp.where(my_core == 0, out_weight[:, :cols], out_weight[:, cols:])
    out_mine = lax.all_gather(out_half, "tensor", axis=0, tiled=True)
    value = jnp.dot(piece, value_weight, preferred_element_type=jnp.float32)
    gate = jnp.dot(piece, gate_weight, preferred_element_type=jnp.float32)
    glu = (value * jax.nn.sigmoid(gate) * valid[:, None]).astype(jnp.bfloat16)
    ff_mine, glu = gather_torus(up_weight, down_weight.T, "tm", glu)
    padded = extended(glu, (("tm", 0),), KERNEL // 2)
    conv = jnp.zeros(glu.shape, jnp.float32)
    for tap in range(KERNEL):
        conv = conv + padded[tap : tap + block].astype(jnp.float32) * depth_kernel[tap]
    count_local = jnp.sum(valid)
    local_sum = jnp.sum(conv * valid[:, None], axis=0)
    local_mean = jnp.where(count_local > 0, local_sum / jnp.maximum(count_local, 1.0), 0.0)
    local_m2 = jnp.sum(jnp.square(conv - local_mean) * valid[:, None], axis=0)
    stats = jnp.stack([jnp.broadcast_to(count_local, local_sum.shape), local_mean, local_m2])
    stats = moments_over(stats, "tm")
    count, mean, m2 = stats[0], stats[1], stats[2]
    centred = conv - mean
    var = m2 / count
    scaled = centred * lax.rsqrt(var + 1e-05) * batch_gain + batch_bias
    swished = (scaled * jax.nn.sigmoid(scaled)).astype(jnp.bfloat16)
    swished_all = lax.all_gather(swished, "tensor", axis=1, tiled=True)
    swap = [(i, i ^ 1) for i in range(lax.axis_size("tm"))]
    out_other, ff_other = lax.ppermute(jnp.stack([out_mine, ff_mine]), "tm", swap)
    up_whole = jnp.where(my_core == 0, ff_mine, ff_other)
    down_t = jnp.where(my_core == 0, ff_other, ff_mine)
    left = jnp.where(my_core == 0, out_mine, out_other)
    right = jnp.where(my_core == 0, out_other, out_mine)
    contract = (((1,), (0,)), ((), ()))
    conv_out = jnp.concatenate(
        [
            lax.dot_general(swished_all, left, contract, preferred_element_type=jnp.float32),
            lax.dot_general(swished_all, right, contract, preferred_element_type=jnp.float32),
        ],
        axis=1,
    )
    mid_block = (feature_block.astype(jnp.float32) + conv_out).astype(jnp.bfloat16)
    mid_block, up_whole, down_t = lax.optimization_barrier((mid_block, up_whole, down_t))
    feed_block = layer_norm(mid_block, feed_gain).astype(jnp.bfloat16)
    mid = lax.dynamic_slice_in_dim(mid_block, lax.axis_index("tensor") * own_rows, own_rows, axis=0)
    pre = jnp.dot(feed_block, up_whole, preferred_element_type=jnp.float32)
    hidden = lax.optimization_barrier((pre * jax.nn.sigmoid(pre)).astype(jnp.bfloat16))
    partial_out = lax.dot_general(
        hidden, down_t, (((1,), (1,)), ((), ())), preferred_element_type=jnp.float32
    )
    feed_out = lax.psum_scatter(
        partial_out.astype(jnp.bfloat16), "tensor", scatter_dimension=0, tiled=True
    ).astype(jnp.float32)
    return (mid.astype(jnp.float32) + 0.5 * feed_out).astype(jnp.bfloat16)


def solution(mesh):
    placed = (
        P(("tm", "tensor"), None),
        P("tm"),
        P(),
        P(),
        P(None, "tensor"),
        P(None, "tensor"),
        P(None, "tensor"),
        P("tensor"),
        P("tensor"),
        P("tensor", None),
        P(),
        P("tm", "tensor"),
        P("tensor", "tm"),
    )
    return jax.shard_map(
        shards, mesh=mesh, in_specs=placed, out_specs=P(("tm", "tensor"), None), check_vma=False
    )
```

```python
import jax
import jax.numpy as jnp
from jax import lax
from jax.experimental.layout import Layout, with_layout_constraint
from jax.sharding import PartitionSpec as P

KERNEL = 31


def extended(array, sides, width):
    for axis, dim in sides:
        devices, length = (lax.axis_size(axis), array.shape[dim])
        up = [(i, (i + 1) % devices) for i in range(devices - 1)]
        down = [(j, i) for i, j in up]
        last = lax.slice_in_dim(array, length - width, length, axis=dim)
        initial = lax.slice_in_dim(array, 0, width, axis=dim)
        before = lax.ppermute(last, axis, up)
        after = lax.ppermute(initial, axis, down)
        array = jnp.concatenate([before, array, after], axis=dim)
    return array


def layer_norm(rows, gain):
    values = rows.astype(jnp.float32)
    centre = jnp.mean(values, axis=-1, keepdims=True)
    spread = jnp.mean(jnp.square(values - centre), axis=-1, keepdims=True)
    return (values - centre) * lax.rsqrt(spread + 1e-05) * gain


def merge_moments(low, high):
    n_a, mean_a, m2_a = low[0], low[1], low[2]
    n_b, mean_b, m2_b = high[0], high[1], high[2]
    n = n_a + n_b
    share = jnp.where(n > 0, n_b / jnp.maximum(n, 1.0), 0.0)
    delta = mean_b - mean_a
    mean = mean_a + delta * share
    m2 = m2_a + m2_b + jnp.square(delta) * n_a * share
    return jnp.stack([n, mean, m2])


def moments_over(stats, axis):
    size = lax.axis_size(axis)
    me = lax.axis_index(axis)
    step = 1
    while step < size:
        pairs = [(i, i ^ step) for i in range(size)]
        other = lax.ppermute(stats, axis, pairs)
        mine_low = (me & step) == 0
        low = jnp.where(mine_low, stats, other)
        high = jnp.where(mine_low, other, stats)
        stats = merge_moments(low, high)
        step *= 2
    return stats


def gather_torus(up_piece, down_piece, axis, tie):
    size = lax.axis_size(axis)
    cores, xs = 2, 4
    ys = size // (cores * xs)

    def coords(i):
        return i // (cores * xs), (i // cores) % xs, i % cores

    def index(y, x, c):
        return (y * xs + x) * cores + c

    me = lax.axis_index(axis)
    my_c = me % cores
    my_x = (me // cores) % xs
    my_y = me // (cores * xs)

    def shifted(value, move):
        pairs = []
        for i in range(size):
            y, x, c = coords(i)
            pairs.append((i, index(*move(y, x, c))))
        return lax.ppermute(value, axis, pairs)

    def ordered(own, received, mine, count):
        slots = [own] + received
        picks = []
        for j in range(count):
            k = (mine - j) % count
            picked = slots[0]
            for t in range(1, count):
                picked = jnp.where(k == t, slots[t], picked)
            picks.append(picked)
        return picks

    partner = lambda y, x, c: (y, x, 1 - c)
    other = shifted(jnp.stack([up_piece, down_piece]), partner)
    other_up, other_down = other[0], other[1]
    pair_up = jnp.concatenate(ordered(up_piece, [other_up], my_c, cores), axis=0)
    pair_down = jnp.concatenate(ordered(down_piece, [other_down], my_c, cores), axis=0)
    pair = jnp.where(my_c == 0, pair_up, pair_down)
    got = [shifted(pair, lambda y, x, c, d=d: (y, (x + d) % xs, c)) for d in range(1, xs)]
    row = jnp.concatenate(ordered(pair, got, my_x, xs), axis=0)
    got = [shifted(row, lambda y, x, c, d=d: ((y + d) % ys, x, c)) for d in range(1, ys)]
    whole = jnp.concatenate(ordered(row, got, my_y, ys), axis=0)
    whole, tie = lax.optimization_barrier((whole, tie))
    return whole, tie


def shards(
    features,
    frame_mask,
    total_length,
    norm_gain,
    value_weight,
    gate_weight,
    depth_kernel,
    batch_gain,
    batch_bias,
    out_weight,
    feed_gain,
    up_weight,
    down_weight,
):
    own_rows = features.shape[0]
    block = own_rows * lax.axis_size("tensor")
    positions = lax.axis_index("tm") * block + jnp.arange(block, dtype=jnp.int32)
    valid = ((frame_mask > 0) & (positions < total_length[0])).astype(jnp.float32)
    feature_block = lax.all_gather(features, "tensor", axis=0, tiled=True)
    feature_block = with_layout_constraint(feature_block, Layout(major_to_minor=(0, 1)))
    piece = layer_norm(feature_block, norm_gain).astype(jnp.bfloat16)
    my_core = lax.axis_index("tm") % 2
    cols = out_weight.shape[1] // 2
    out_half = jnp.where(my_core == 0, out_weight[:, :cols], out_weight[:, cols:])
    out_mine = lax.all_gather(out_half, "tensor", axis=0, tiled=True)
    value = jnp.dot(piece, value_weight, preferred_element_type=jnp.float32)
    gate = jnp.dot(piece, gate_weight, preferred_element_type=jnp.float32)
    glu = (value * jax.nn.sigmoid(gate) * valid[:, None]).astype(jnp.bfloat16)
    ff_mine, glu = gather_torus(up_weight, down_weight.T, "tm", glu)
    padded = extended(glu, (("tm", 0),), KERNEL // 2)
    conv = jnp.zeros(glu.shape, jnp.float32)
    for tap in range(KERNEL):
        conv = conv + padded[tap : tap + block].astype(jnp.float32) * depth_kernel[tap]
    conv = lax.optimization_barrier(conv)
    count_local = jnp.sum(valid)
    local_sum = jnp.sum(conv * valid[:, None], axis=0)
    local_mean = jnp.where(count_local > 0, local_sum / jnp.maximum(count_local, 1.0), 0.0)
    local_m2 = jnp.sum(jnp.square(conv - local_mean) * valid[:, None], axis=0)
    stats = jnp.stack([jnp.broadcast_to(count_local, local_sum.shape), local_mean, local_m2])
    stats = moments_over(stats, "tm")
    count, mean, m2 = stats[0], stats[1], stats[2]
    centred = conv - mean
    var = m2 / count
    scaled = centred * lax.rsqrt(var + 1e-05) * batch_gain + batch_bias
    swished = (scaled * jax.nn.sigmoid(scaled)).astype(jnp.bfloat16)
    swished_all = lax.all_gather(swished, "tensor", axis=1, tiled=True)
    swap = [(i, i ^ 1) for i in range(lax.axis_size("tm"))]
    out_other, ff_other = lax.ppermute(jnp.stack([out_mine, ff_mine]), "tm", swap)
    up_whole = jnp.where(my_core == 0, ff_mine, ff_other)
    down_t = jnp.where(my_core == 0, ff_other, ff_mine)
    left = jnp.where(my_core == 0, out_mine, out_other)
    right = jnp.where(my_core == 0, out_other, out_mine)
    contract = (((1,), (0,)), ((), ()))
    conv_out = jnp.concatenate(
        [
            lax.dot_general(swished_all, left, contract, preferred_element_type=jnp.float32),
            lax.dot_general(swished_all, right, contract, preferred_element_type=jnp.float32),
        ],
        axis=1,
    )
    mid_block = (feature_block.astype(jnp.float32) + conv_out).astype(jnp.bfloat16)
    mid_block, up_whole, down_t = lax.optimization_barrier((mid_block, up_whole, down_t))
    feed_block = layer_norm(mid_block, feed_gain).astype(jnp.bfloat16)
    mid = lax.dynamic_slice_in_dim(mid_block, lax.axis_index("tensor") * own_rows, own_rows, axis=0)
    pre = jnp.dot(feed_block, up_whole, preferred_element_type=jnp.float32)
    hidden = lax.optimization_barrier((pre * jax.nn.sigmoid(pre)).astype(jnp.bfloat16))
    partial_out = lax.dot_general(
        hidden, down_t, (((1,), (1,)), ((), ())), preferred_element_type=jnp.float32
    )
    feed_out = lax.psum_scatter(
        partial_out.astype(jnp.bfloat16), "tensor", scatter_dimension=0, tiled=True
    ).astype(jnp.float32)
    return (mid.astype(jnp.float32) + 0.5 * feed_out).astype(jnp.bfloat16)


def solution(mesh):
    placed = (
        P(("tm", "tensor"), None),
        P("tm"),
        P(),
        P(),
        P(None, "tensor"),
        P(None, "tensor"),
        P(None, "tensor"),
        P("tensor"),
        P("tensor"),
        P("tensor", None),
        P(),
        P("tm", "tensor"),
        P("tensor", "tm"),
    )
    return jax.shard_map(
        shards, mesh=mesh, in_specs=placed, out_specs=P(("tm", "tensor"), None), check_vma=False
    )
```

```python
import jax
import jax.numpy as jnp
from jax import lax
from jax.experimental.layout import Layout, with_layout_constraint
from jax.sharding import PartitionSpec as P

KERNEL = 31


def extended(array, sides, width):
    for axis, dim in sides:
        devices, length = (lax.axis_size(axis), array.shape[dim])
        up = [(i, (i + 1) % devices) for i in range(devices - 1)]
        down = [(j, i) for i, j in up]
        last = lax.slice_in_dim(array, length - width, length, axis=dim)
        initial = lax.slice_in_dim(array, 0, width, axis=dim)
        before = lax.ppermute(last, axis, up)
        after = lax.ppermute(initial, axis, down)
        array = jnp.concatenate([before, array, after], axis=dim)
    return array


def layer_norm(rows, gain):
    values = rows.astype(jnp.float32)
    centre = jnp.mean(values, axis=-1, keepdims=True)
    spread = jnp.mean(jnp.square(values - centre), axis=-1, keepdims=True)
    return (values - centre) * lax.rsqrt(spread + 1e-05) * gain


def merge_moments(low, high):
    n_a, mean_a, m2_a = low[0], low[1], low[2]
    n_b, mean_b, m2_b = high[0], high[1], high[2]
    n = n_a + n_b
    share = jnp.where(n > 0, n_b / jnp.maximum(n, 1.0), 0.0)
    delta = mean_b - mean_a
    mean = mean_a + delta * share
    m2 = m2_a + m2_b + jnp.square(delta) * n_a * share
    return jnp.stack([n, mean, m2])


def moments_over(stats, axis):
    size = lax.axis_size(axis)
    me = lax.axis_index(axis)
    step = 1
    while step < size:
        pairs = [(i, i ^ step) for i in range(size)]
        other = lax.ppermute(stats, axis, pairs)
        mine_low = (me & step) == 0
        low = jnp.where(mine_low, stats, other)
        high = jnp.where(mine_low, other, stats)
        stats = merge_moments(low, high)
        step *= 2
    return stats


def gather_torus(up_piece, down_piece, axis, tie):
    size = lax.axis_size(axis)
    cores, xs = 2, 4
    ys = size // (cores * xs)

    def coords(i):
        return i // (cores * xs), (i // cores) % xs, i % cores

    def index(y, x, c):
        return (y * xs + x) * cores + c

    me = lax.axis_index(axis)
    my_c = me % cores
    my_x = (me // cores) % xs
    my_y = me // (cores * xs)

    def shifted(value, move):
        pairs = []
        for i in range(size):
            y, x, c = coords(i)
            pairs.append((i, index(*move(y, x, c))))
        return lax.ppermute(value, axis, pairs)

    def ordered(own, received, mine, count):
        slots = [own] + received
        picks = []
        for j in range(count):
            k = (mine - j) % count
            picked = slots[0]
            for t in range(1, count):
                picked = jnp.where(k == t, slots[t], picked)
            picks.append(picked)
        return picks

    partner = lambda y, x, c: (y, x, 1 - c)
    other = shifted(jnp.stack([up_piece, down_piece]), partner)
    other_up, other_down = other[0], other[1]
    pair_up = jnp.concatenate(ordered(up_piece, [other_up], my_c, cores), axis=0)
    pair_down = jnp.concatenate(ordered(down_piece, [other_down], my_c, cores), axis=0)
    pair = jnp.where(my_c == 0, pair_up, pair_down)
    got = [shifted(pair, lambda y, x, c, d=d: (y, (x + d) % xs, c)) for d in range(1, xs)]
    row = jnp.concatenate(ordered(pair, got, my_x, xs), axis=0)
    got = [shifted(row, lambda y, x, c, d=d: ((y + d) % ys, x, c)) for d in range(1, ys)]
    whole = jnp.concatenate(ordered(row, got, my_y, ys), axis=0)
    whole, tie = lax.optimization_barrier((whole, tie))
    return whole, tie


def shards(
    features,
    frame_mask,
    total_length,
    norm_gain,
    value_weight,
    gate_weight,
    depth_kernel,
    batch_gain,
    batch_bias,
    out_weight,
    feed_gain,
    up_weight,
    down_weight,
):
    own_rows = features.shape[0]
    block = own_rows * lax.axis_size("tensor")
    positions = lax.axis_index("tm") * block + jnp.arange(block, dtype=jnp.int32)
    valid = ((frame_mask > 0) & (positions < total_length[0])).astype(jnp.float32)
    feature_block = lax.all_gather(features, "tensor", axis=0, tiled=True)
    feature_block = with_layout_constraint(feature_block, Layout(major_to_minor=(0, 1)))
    piece = layer_norm(feature_block, norm_gain).astype(jnp.bfloat16)
    my_core = lax.axis_index("tm") % 2
    cols = out_weight.shape[1] // 2
    out_half = jnp.where(my_core == 0, out_weight[:, :cols], out_weight[:, cols:])
    out_mine = lax.all_gather(out_half, "tensor", axis=0, tiled=True)
    value = jnp.dot(piece, value_weight, preferred_element_type=jnp.float32)
    gate = jnp.dot(piece, gate_weight, preferred_element_type=jnp.float32)
    value, gate = lax.optimization_barrier((value, gate))
    glu = (value * jax.nn.sigmoid(gate) * valid[:, None]).astype(jnp.bfloat16)
    ff_mine, glu = gather_torus(up_weight, down_weight.T, "tm", glu)
    padded = extended(glu, (("tm", 0),), KERNEL // 2)
    conv = jnp.zeros(glu.shape, jnp.float32)
    for tap in range(KERNEL):
        conv = conv + padded[tap : tap + block].astype(jnp.float32) * depth_kernel[tap]
    count_local = jnp.sum(valid)
    local_sum = jnp.sum(conv * valid[:, None], axis=0)
    local_mean = jnp.where(count_local > 0, local_sum / jnp.maximum(count_local, 1.0), 0.0)
    local_m2 = jnp.sum(jnp.square(conv - local_mean) * valid[:, None], axis=0)
    stats = jnp.stack([jnp.broadcast_to(count_local, local_sum.shape), local_mean, local_m2])
    stats = moments_over(stats, "tm")
    count, mean, m2 = stats[0], stats[1], stats[2]
    centred = conv - mean
    var = m2 / count
    scaled = centred * lax.rsqrt(var + 1e-05) * batch_gain + batch_bias
    swished = (scaled * jax.nn.sigmoid(scaled)).astype(jnp.bfloat16)
    swished_all = lax.all_gather(swished, "tensor", axis=1, tiled=True)
    swap = [(i, i ^ 1) for i in range(lax.axis_size("tm"))]
    out_other, ff_other = lax.ppermute(jnp.stack([out_mine, ff_mine]), "tm", swap)
    up_whole = jnp.where(my_core == 0, ff_mine, ff_other)
    down_t = jnp.where(my_core == 0, ff_other, ff_mine)
    left = jnp.where(my_core == 0, out_mine, out_other)
    right = jnp.where(my_core == 0, out_other, out_mine)
    contract = (((1,), (0,)), ((), ()))
    conv_out = jnp.concatenate(
        [
            lax.dot_general(swished_all, left, contract, preferred_element_type=jnp.float32),
            lax.dot_general(swished_all, right, contract, preferred_element_type=jnp.float32),
        ],
        axis=1,
    )
    mid_block = (feature_block.astype(jnp.float32) + conv_out).astype(jnp.bfloat16)
    mid_block, up_whole, down_t = lax.optimization_barrier((mid_block, up_whole, down_t))
    feed_block = layer_norm(mid_block, feed_gain).astype(jnp.bfloat16)
    mid = lax.dynamic_slice_in_dim(mid_block, lax.axis_index("tensor") * own_rows, own_rows, axis=0)
    pre = jnp.dot(feed_block, up_whole, preferred_element_type=jnp.float32)
    hidden = lax.optimization_barrier((pre * jax.nn.sigmoid(pre)).astype(jnp.bfloat16))
    partial_out = lax.dot_general(
        hidden, down_t, (((1,), (1,)), ((), ())), preferred_element_type=jnp.float32
    )
    feed_out = lax.psum_scatter(
        partial_out.astype(jnp.bfloat16), "tensor", scatter_dimension=0, tiled=True
    ).astype(jnp.float32)
    return (mid.astype(jnp.float32) + 0.5 * feed_out).astype(jnp.bfloat16)


def solution(mesh):
    placed = (
        P(("tm", "tensor"), None),
        P("tm"),
        P(),
        P(),
        P(None, "tensor"),
        P(None, "tensor"),
        P(None, "tensor"),
        P("tensor"),
        P("tensor"),
        P("tensor", None),
        P(),
        P("tm", "tensor"),
        P("tensor", "tm"),
    )
    return jax.shard_map(
        shards, mesh=mesh, in_specs=placed, out_specs=P(("tm", "tensor"), None), check_vma=False
    )
```
